512 devices in a mesh: tensor: 16 (over z_lo, x, core), dp: 32 (over y, z_hi).
Axes of the slice: x: 4, y: 8, z: 8 (z_hi: 4, z_lo: 2; z = z_hi * 2 + z_lo), core: 2. Of those that a mesh axis runs over, the one named last changes fastest.
Arguments:
- activations: bfloat16 [4096, 4096], P('dp', 'tensor'), may hold values from -6 to 6
- out_grad: bfloat16 [4096, 4096], P('dp', 'tensor'), may hold values from -6 to 6
- up_blocks: bfloat16 [1024, 128, 128], P(('tensor', 'dp')), may hold values from -0.1875 to 0.1875
- up_rows: int32 [1024], P('tensor'), may hold values from 0 to 31, as said below
- down_blocks: bfloat16 [1024, 128, 128], P(('tensor', 'dp')), may hold values from -0.09375 to 0.09375
- down_rows: int32 [1024], P('tensor'), may hold values from 0 to 31, as said below
Outputs:
- output: bfloat16 [4096, 4096], P('dp')
- input_grad: bfloat16 [4096, 4096], P('dp')
- up_grad: bfloat16 [1024, 128, 128], P(('tensor', 'dp'))
- down_grad: bfloat16 [1024, 128, 128], P(('tensor', 'dp'))
The draws below stay inside these ranges and needn't reach their ends.
Inputs may be any that keep to these rules, and one draw needn't show every extreme that they name: `up_rows`: entry b is the input row block of up block b, whose hidden block is b // 8; the 8 entries of one hidden block are distinct; every row block is named by 32 entries. `down_rows`: entry b is the output block of down block b, whose hidden block is b // 8; the 8 entries of one hidden block are distinct; every output block is named by 32 entries.
All inputs are finite; a program needn't handle non-finite values.
Results may differ from the reference program's by a relative error of at most 0.022.
Values may be sent and summed in bfloat16 or wider, within the bound.
No kernel may reach another device: no remote copies, remote signals or barrier semaphores. Data moves between devices by JAX's collectives and lax.ppermute only.
A program may use at most 64 MiB of HBM per device.

```python
import math
import jax
import jax.numpy as jnp
from jax import lax

D = 4096
BLK = 128
K = 8
TOK_DEV = 128
R = 32
C = 128
NBLK = 1024
TOKENS = 4096
N_TENSOR = 16
N_DP = 32


def butterfly_rows(key):
    first_key, second_key = jax.random.split(key)
    strides = jnp.concatenate([jnp.zeros((1,), jnp.int32), jax.random.permutation(first_key, R - 1)[:K - 1].astype(jnp.int32) + 1])
    offset_value = jax.random.randint(second_key, (), 0, R).astype(jnp.int32)
    anchor = (jnp.arange(C, dtype=jnp.int32) + offset_value) % R
    return jnp.bitwise_xor(anchor[:, None], strides[None, :]).reshape(NBLK).astype(jnp.int32)


def draw_up_rows(key, part):
    return butterfly_rows(jax.random.fold_in(key, 3))


def draw_down_rows(key, part):
    return butterfly_rows(jax.random.fold_in(key, 5))


def levels(own_key, dims, cuts, least, largest):
    loudness = 1.0
    for dim, blocks in cuts:
        heights = jax.random.uniform(jax.random.fold_in(jax.random.fold_in(own_key, 6), dim), (blocks,), jnp.float32, least / len(cuts), largest / len(cuts))
        loudness = loudness * jnp.repeat(jnp.exp(heights), dims[dim] // blocks).reshape((-1,) + (1,) * (len(dims) - 1 - dim))
    return loudness


def scatter_about(key, extent, scale, reach, cuts=(), held_as=jnp.bfloat16):
    array = jax.random.normal(key, extent, jnp.float32) * scale
    if len(cuts) > 0:
        array = levels(key, extent, cuts, -0.22, 0.18) * array
    return jnp.clip(array, min=-reach, max=reach).astype(held_as)


def setup_inputs(seed: int = 0) -> dict:
    seeds = jax.random.split(jax.random.key(seed), 7)
    return {
        "activations": scatter_about(seeds[0], (TOKENS, D), 1.0, 6.0, ((0, 32), (1, 16))),
        "out_grad": scatter_about(seeds[1], (TOKENS, D), 1.0, 6.0, ((0, 32), (1, 16))),
        "up_blocks": scatter_about(seeds[2], (NBLK, BLK, BLK), (K * BLK) ** -0.5, 0.1875, ((0, 512),)),
        "up_rows": draw_up_rows(jax.random.fold_in(seeds[6], 71), 0),
        "down_blocks": scatter_about(seeds[4], (NBLK, BLK, BLK), (NBLK // R * BLK) ** -0.5, 0.09375, ((0, 512),)),
        "down_rows": draw_down_rows(jax.random.fold_in(seeds[6], 71), 0),
    }


def normal_cdf(value):
    return 0.5 * (1.0 + jax.scipy.special.erf(value * 0.7071067811865476))

def gelu_slope(value):
    return normal_cdf(value) + value * jnp.exp(-0.5 * value * value) * 0.3989422804014327

def rounded(value):
    return lax.optimization_barrier(value.astype(jnp.bfloat16)).astype(jnp.float32)

def reference(activations, out_grad, up_blocks, up_rows, down_blocks, down_rows):
    groups = C // N_TENSOR
    scale = 1.0 / math.sqrt(TOKENS)
    in_split = activations.astype(jnp.float32).reshape(TOKENS, R, BLK)
    grad_split = out_grad.astype(jnp.float32).reshape(TOKENS, R, BLK)
    up_tiles = up_blocks.astype(jnp.float32).reshape(N_TENSOR, groups, K, BLK, BLK)
    down_tiles = down_blocks.astype(jnp.float32).reshape(N_TENSOR, groups, K, BLK, BLK)
    up_index = up_rows.astype(jnp.int32).reshape(N_TENSOR, groups, K)
    down_index = down_rows.astype(jnp.int32).reshape(N_TENSOR, groups, K)
    span = jnp.arange(R, dtype=jnp.int32)
    highest = lax.Precision.HIGHEST

    def member(carry, item):
        out_total, in_total = carry
        up_group, up_group_rows, down_group, down_group_rows = item
        picked_in = in_split[:, up_group_rows]
        preact = jnp.einsum('tgki,gkio->tgo', picked_in, up_group)
        hidden = rounded(preact * normal_cdf(preact))
        product = jnp.einsum('tgh,gkho->tgko', hidden, down_group)
        down_onehot = (down_group_rows[..., None] == span).astype(jnp.float32)
        out_part = jnp.einsum('tgko,gkr->tro', product, down_onehot, precision=highest).reshape(TOKENS, D)
        picked_grad = grad_split[:, down_group_rows]
        hidden_grad = jnp.einsum('tgko,gkho->tgh', picked_grad, down_group)
        preact_grad = rounded(hidden_grad * gelu_slope(preact))
        back = jnp.einsum('tgo,gkio->tgki', preact_grad, up_group)
        up_onehot = (up_group_rows[..., None] == span).astype(jnp.float32)
        in_part = jnp.einsum('tgki,gkr->tri', back, up_onehot, precision=highest).reshape(TOKENS, D)
        up_term = jnp.einsum('ntgki,ntgo->ngkio', picked_in.reshape(N_DP, TOK_DEV, groups, K, BLK), preact_grad.reshape(N_DP, TOK_DEV, groups, BLK)) * scale
        down_term = jnp.einsum('ntgh,ntgko->ngkho', hidden.reshape(N_DP, TOK_DEV, groups, BLK), picked_grad.reshape(N_DP, TOK_DEV, groups, K, BLK)) * scale
        up_sum = lax.optimization_barrier(jnp.sum(rounded(up_term), axis=0)).astype(jnp.bfloat16)
        down_sum = lax.optimization_barrier(jnp.sum(rounded(down_term), axis=0)).astype(jnp.bfloat16)
        return ((out_total + rounded(out_part), in_total + rounded(in_part)), (up_sum, down_sum))
    start = (jnp.zeros((TOKENS, D), jnp.float32), jnp.zeros((TOKENS, D), jnp.float32))
    totals, grads = lax.scan(member, start, (up_tiles, up_index, down_tiles, down_index))
    output = totals[0].astype(jnp.bfloat16)
    input_grad = totals[1].astype(jnp.bfloat16)
    up_grad = grads[0].reshape(NBLK, BLK, BLK)
    down_grad = grads[1].reshape(NBLK, BLK, BLK)
    return (output, input_grad, up_grad, down_grad)
```

```python
import math

import jax
import jax.numpy as jnp
from jax import lax
from jax.sharding import PartitionSpec as P

K = 8


def normal_cdf(value):
    return 0.5 * (1.0 + jax.scipy.special.erf(value * 0.7071067811865476))


def gelu_slope(value):
    return normal_cdf(value) + value * jnp.exp(-0.5 * value * value) * 0.3989422804014327


def gather_all(x, axis_name):
    n = lax.axis_size(axis_name)
    spread = jnp.broadcast_to(x[None], (n,) + x.shape)
    return lax.all_to_all(spread, axis_name, 0, 0, tiled=True)


def scatter_sum(x, axis_name):
    got = lax.all_to_all(x, axis_name, 0, 0, tiled=True)
    return got.astype(jnp.float32).sum(axis=0).astype(jnp.bfloat16)


def per_device(activations, out_grad, up_blocks, up_rows, down_blocks, down_rows):
    block_size = up_blocks.shape[1]
    groups = up_rows.shape[0] // K
    n_tensor = lax.axis_size("tensor")
    n_dp = lax.axis_size("dp")
    tokens = activations.shape[0]
    shard_width = activations.shape[1]
    width = shard_width * n_tensor
    row_blocks = width // block_size

    feats = gather_all(jnp.stack([activations, out_grad]), "tensor")
    feats = jnp.moveaxis(feats, 0, 2).reshape(2, tokens, width)
    full_input, full_grad = feats[0], feats[1]
    weights = gather_all(jnp.stack([up_blocks, down_blocks]), "dp")
    weights = jnp.moveaxis(weights, 1, 0).reshape(2, -1, block_size, block_size)
    up_all, down_all = weights[0], weights[1]

    scale = 1.0 / math.sqrt(tokens * n_dp)
    up_tiles = up_all.reshape(groups, K, block_size, block_size)
    down_tiles = down_all.reshape(groups, K, block_size, block_size)
    up_index = up_rows.reshape(groups, K)
    down_index = down_rows.reshape(groups, K)
    picked_in = full_input.reshape(tokens, row_blocks, block_size)[:, up_index]
    preact = jnp.einsum("tgki,gkio->tgo", picked_in, up_tiles, preferred_element_type=jnp.float32)
    hidden = (preact * normal_cdf(preact)).astype(jnp.bfloat16)
    product = jnp.einsum("tgh,gkho->tgko", hidden, down_tiles, preferred_element_type=jnp.float32)
    out_start = jnp.zeros((tokens, row_blocks, block_size), jnp.float32)
    out_part = out_start.at[:, down_rows].add(product.reshape(tokens, groups * K, block_size))
    picked_grad = full_grad.reshape(tokens, row_blocks, block_size)[:, down_index]
    down_term = (
        jnp.einsum("tgh,tgko->gkho", hidden, picked_grad, preferred_element_type=jnp.float32)
        * scale
    )
    hidden_grad = jnp.einsum(
        "tgko,gkho->tgh", picked_grad, down_tiles, preferred_element_type=jnp.float32
    )
    preact_grad = (hidden_grad * gelu_slope(preact)).astype(jnp.bfloat16)
    back = jnp.einsum("tgo,gkio->tgki", preact_grad, up_tiles, preferred_element_type=jnp.float32)
    in_start = jnp.zeros((tokens, row_blocks, block_size), jnp.float32)
    in_part = in_start.at[:, up_rows].add(back.reshape(tokens, groups * K, block_size))
    up_term = (
        jnp.einsum("tgki,tgo->gkio", picked_in, preact_grad, preferred_element_type=jnp.float32)
        * scale
    )

    parts = jnp.stack([out_part, in_part]).astype(jnp.bfloat16)
    parts = parts.reshape(2, tokens, n_tensor, shard_width)
    mine = scatter_sum(jnp.moveaxis(parts, 2, 0), "tensor")
    both = gather_all(mine, "tensor")
    both = jnp.moveaxis(both, 0, 2).reshape(2, tokens, width)

    terms = jnp.stack([up_term, down_term]).astype(jnp.bfloat16)
    terms = terms.reshape(2, n_dp, -1, block_size, block_size)
    grads = scatter_sum(jnp.moveaxis(terms, 1, 0), "dp")
    return (both[0], both[1], grads[0], grads[1])


def solution(mesh):
    placed = (
        P("dp", "tensor"),
        P("dp", "tensor"),
        P(("tensor", "dp"), None, None),
        P("tensor"),
        P(("tensor", "dp"), None, None),
        P("tensor"),
    )
    return jax.shard_map(
        per_device,
        mesh=mesh,
        in_specs=placed,
        out_specs=(
            P("dp", None),
            P("dp", None),
            P(("tensor", "dp"), None, None),
            P(("tensor", "dp"), None, None),
        ),
        check_vma=False,
    )
```

```python
import math

import jax
import jax.numpy as jnp
from jax import lax
from jax.sharding import PartitionSpec as P

K = 8


def normal_cdf(value):
    return 0.5 * (1.0 + jax.scipy.special.erf(value * 0.7071067811865476))


def gelu_slope(value):
    return normal_cdf(value) + value * jnp.exp(-0.5 * value * value) * 0.3989422804014327


def gather_all(x, axis_name):
    n = lax.axis_size(axis_name)
    spread = jnp.broadcast_to(x[None], (n,) + x.shape)
    return lax.all_to_all(spread, axis_name, 0, 0, tiled=True)


def scatter_sum(x, axis_name):
    got = lax.all_to_all(x, axis_name, 0, 0, tiled=True)
    return got.astype(jnp.float32).sum(axis=0).astype(jnp.bfloat16)


Z_HI = 4


def dp_shift(n_y, n_z, dy, dz):
    return [
        (y * n_z + z, ((y + dy) % n_y) * n_z + (z + dz) % n_z)
        for y in range(n_y)
        for z in range(n_z)
    ]


def dp_gather_rel(x, n_y, n_z):
    by_z = [x] + [lax.ppermute(x, "dp", dp_shift(n_y, n_z, 0, b)) for b in range(1, n_z)]
    held = jnp.stack(by_z)
    n_f, n_b = n_y // 2, (n_y - 1) // 2
    fwd, bwd = [held], []
    cur_f = cur_b = held
    for k in range(1, n_f + 1):
        cur_f = lax.ppermute(cur_f, "dp", dp_shift(n_y, n_z, 1, 0))
        fwd.append(cur_f)
        if k <= n_b:
            cur_b = lax.ppermute(cur_b, "dp", dp_shift(n_y, n_z, -1, 0))
            bwd.append(cur_b)
    rel = fwd + [bwd[n_y - a - 1] for a in range(len(fwd), n_y)]
    return jnp.stack(rel)


def dp_scatter_rel(terms, n_y, n_z):
    n_f, n_b = n_y // 2, (n_y - 1) // 2
    got_f = got_b = None
    for k in range(1, n_f + 1):
        part = terms[(n_y - n_f - 1 + k) % n_y].astype(jnp.float32)
        if got_f is not None:
            part = part + got_f.astype(jnp.float32)
        got_f = lax.ppermute(part.astype(jnp.bfloat16), "dp", dp_shift(n_y, n_z, 1, 0))
    for k in range(1, n_b + 1):
        part = terms[n_b + 1 - k].astype(jnp.float32)
        if got_b is not None:
            part = part + got_b.astype(jnp.float32)
        got_b = lax.ppermute(part.astype(jnp.bfloat16), "dp", dp_shift(n_y, n_z, -1, 0))
    acc = terms[0].astype(jnp.float32)
    if got_f is not None:
        acc = acc + got_f.astype(jnp.float32)
    if got_b is not None:
        acc = acc + got_b.astype(jnp.float32)
    total = acc[0]
    for b in range(1, n_z):
        sent = lax.ppermute(acc[b].astype(jnp.bfloat16), "dp", dp_shift(n_y, n_z, 0, -b))
        total = total + sent.astype(jnp.float32)
    return total.astype(jnp.bfloat16)


def per_device(activations, out_grad, up_blocks, up_rows, down_blocks, down_rows):
    block_size = up_blocks.shape[1]
    groups = up_rows.shape[0] // K
    n_tensor = lax.axis_size("tensor")
    n_dp = lax.axis_size("dp")
    tokens = activations.shape[0]
    shard_width = activations.shape[1]
    width = shard_width * n_tensor
    row_blocks = width // block_size

    feats = gather_all(jnp.stack([activations, out_grad]), "tensor")
    feats = jnp.moveaxis(feats, 0, 2).reshape(2, tokens, width)
    full_input, full_grad = feats[0], feats[1]
    per_dev = up_blocks.shape[0]
    n_z = Z_HI
    n_y = n_dp // n_z
    if n_z * per_dev != K:
        raise ValueError("layout")
    weights = dp_gather_rel(jnp.stack([up_blocks, down_blocks]), n_y, n_z)
    weights = jnp.moveaxis(weights, 2, 0).reshape(2, -1, block_size, block_size)
    up_all, down_all = weights[0], weights[1]
    me = lax.axis_index("dp")
    my_y, my_z = me // n_z, me % n_z
    a = jnp.arange(n_y, dtype=jnp.int32)[:, None, None]
    b = jnp.arange(n_z, dtype=jnp.int32)[None, :, None]
    r = jnp.arange(per_dev, dtype=jnp.int32)[None, None, :]
    order = ((((my_y - a) % n_y) * n_z + (my_z - b) % n_z) * per_dev + r).reshape(-1)
    up_rows = up_rows[order]
    down_rows = down_rows[order]

    scale = 1.0 / math.sqrt(tokens * n_dp)
    up_tiles = up_all.reshape(groups, K, block_size, block_size)
    down_tiles = down_all.reshape(groups, K, block_size, block_size)
    up_index = up_rows.reshape(groups, K)
    down_index = down_rows.reshape(groups, K)
    picked_in = full_input.reshape(tokens, row_blocks, block_size)[:, up_index]
    preact = jnp.einsum("tgki,gkio->tgo", picked_in, up_tiles, preferred_element_type=jnp.float32)
    hidden = (preact * normal_cdf(preact)).astype(jnp.bfloat16)
    product = jnp.einsum("tgh,gkho->tgko", hidden, down_tiles, preferred_element_type=jnp.float32)
    out_start = jnp.zeros((tokens, row_blocks, block_size), jnp.float32)
    out_part = out_start.at[:, down_rows].add(product.reshape(tokens, groups * K, block_size))
    picked_grad = full_grad.reshape(tokens, row_blocks, block_size)[:, down_index]
    down_term = (
        jnp.einsum("tgh,tgko->gkho", hidden, picked_grad, preferred_element_type=jnp.float32)
        * scale
    )
    hidden_grad = jnp.einsum(
        "tgko,gkho->tgh", picked_grad, down_tiles, preferred_element_type=jnp.float32
    )
    preact_grad = (hidden_grad * gelu_slope(preact)).astype(jnp.bfloat16)
    back = jnp.einsum("tgo,gkio->tgki", preact_grad, up_tiles, preferred_element_type=jnp.float32)
    in_start = jnp.zeros((tokens, row_blocks, block_size), jnp.float32)
    in_part = in_start.at[:, up_rows].add(back.reshape(tokens, groups * K, block_size))
    up_term = (
        jnp.einsum("tgki,tgo->gkio", picked_in, preact_grad, preferred_element_type=jnp.float32)
        * scale
    )

    parts = jnp.stack([out_part, in_part]).astype(jnp.bfloat16)
    parts = parts.reshape(2, tokens, n_tensor, shard_width)
    mine = scatter_sum(jnp.moveaxis(parts, 2, 0), "tensor")
    both = gather_all(mine, "tensor")
    both = jnp.moveaxis(both, 0, 2).reshape(2, tokens, width)

    terms = jnp.stack([up_term, down_term]).astype(jnp.bfloat16)
    terms = terms.reshape(2, n_y, n_z, per_dev, block_size, block_size)
    grads = dp_scatter_rel(jnp.moveaxis(terms, 0, 2), n_y, n_z)
    return (both[0], both[1], grads[0], grads[1])


def solution(mesh):
    placed = (
        P("dp", "tensor"),
        P("dp", "tensor"),
        P(("tensor", "dp"), None, None),
        P("tensor"),
        P(("tensor", "dp"), None, None),
        P("tensor"),
    )
    return jax.shard_map(
        per_device,
        mesh=mesh,
        in_specs=placed,
        out_specs=(
            P("dp", None),
            P("dp", None),
            P(("tensor", "dp"), None, None),
            P(("tensor", "dp"), None, None),
        ),
        check_vma=False,
    )
```

```python
import math

import jax
import jax.numpy as jnp
from jax import lax
from jax.sharding import PartitionSpec as P

K = 8


def normal_cdf(value):
    return 0.5 * (1.0 + jax.scipy.special.erf(value * 0.7071067811865476))


def gelu_slope(value):
    return normal_cdf(value) + value * jnp.exp(-0.5 * value * value) * 0.3989422804014327


def gather_all(x, axis_name):
    n = lax.axis_size(axis_name)
    spread = jnp.broadcast_to(x[None], (n,) + x.shape)
    return lax.all_to_all(spread, axis_name, 0, 0, tiled=True)


def scatter_sum(x, axis_name):
    got = lax.all_to_all(x, axis_name, 0, 0, tiled=True)
    return got.astype(jnp.float32).sum(axis=0).astype(jnp.bfloat16)


Z_HI = 4


def dp_shift(n_y, n_z, dy, dz):
    return [
        (y * n_z + z, ((y + dy) % n_y) * n_z + (z + dz) % n_z)
        for y in range(n_y)
        for z in range(n_z)
    ]


def dp_gather_rel(x, n_y, n_z):
    by_z = [x] + [lax.ppermute(x, "dp", dp_shift(n_y, n_z, 0, b)) for b in range(1, n_z)]
    held = jnp.stack(by_z)
    n_f, n_b = n_y // 2, (n_y - 1) // 2
    fwd, bwd = [held], []
    cur_f = cur_b = held
    for k in range(1, n_f + 1):
        cur_f = lax.ppermute(cur_f, "dp", dp_shift(n_y, n_z, 1, 0))
        fwd.append(cur_f)
        if k <= n_b:
            cur_b = lax.ppermute(cur_b, "dp", dp_shift(n_y, n_z, -1, 0))
            bwd.append(cur_b)
    rel = fwd + [bwd[n_y - a - 1] for a in range(len(fwd), n_y)]
    return jnp.stack(rel)


def dp_scatter_rel(terms, n_y, n_z):
    n_f, n_b = n_y // 2, (n_y - 1) // 2
    got_f = got_b = None
    for k in range(1, n_f + 1):
        part = terms[(n_y - n_f - 1 + k) % n_y].astype(jnp.float32)
        if got_f is not None:
            part = part + got_f.astype(jnp.float32)
        got_f = lax.ppermute(part.astype(jnp.bfloat16), "dp", dp_shift(n_y, n_z, 1, 0))
    for k in range(1, n_b + 1):
        part = terms[n_b + 1 - k].astype(jnp.float32)
        if got_b is not None:
            part = part + got_b.astype(jnp.float32)
        got_b = lax.ppermute(part.astype(jnp.bfloat16), "dp", dp_shift(n_y, n_z, -1, 0))
    acc = terms[0].astype(jnp.float32)
    if got_f is not None:
        acc = acc + got_f.astype(jnp.float32)
    if got_b is not None:
        acc = acc + got_b.astype(jnp.float32)
    total = acc[0]
    for b in range(1, n_z):
        sent = lax.ppermute(acc[b].astype(jnp.bfloat16), "dp", dp_shift(n_y, n_z, 0, -b))
        total = total + sent.astype(jnp.float32)
    return total.astype(jnp.bfloat16)


def per_device(activations, out_grad, up_blocks, up_rows, down_blocks, down_rows):
    block_size = up_blocks.shape[1]
    groups = up_rows.shape[0] // K
    n_tensor = lax.axis_size("tensor")
    n_dp = lax.axis_size("dp")
    tokens = activations.shape[0]
    shard_width = activations.shape[1]
    width = shard_width * n_tensor
    row_blocks = width // block_size

    feats = gather_all(jnp.stack([activations, out_grad]), "tensor")
    feats = jnp.moveaxis(feats, 0, 2).reshape(2, tokens, width)
    full_input, full_grad = feats[0], feats[1]
    per_dev = up_blocks.shape[0]
    n_z = Z_HI
    n_y = n_dp // n_z
    if n_z * per_dev != K:
        raise ValueError("layout")
    weights = dp_gather_rel(jnp.stack([up_blocks, down_blocks]), n_y, n_z)
    weights = jnp.moveaxis(weights, 2, 0).reshape(2, -1, block_size, block_size)
    up_all, down_all = weights[0], weights[1]
    me = lax.axis_index("dp")
    my_y, my_z = me // n_z, me % n_z
    a = jnp.arange(n_y, dtype=jnp.int32)[:, None, None]
    b = jnp.arange(n_z, dtype=jnp.int32)[None, :, None]
    r = jnp.arange(per_dev, dtype=jnp.int32)[None, None, :]
    order = ((((my_y - a) % n_y) * n_z + (my_z - b) % n_z) * per_dev + r).reshape(-1)
    up_rows = up_rows[order]
    down_rows = down_rows[order]

    scale = 1.0 / math.sqrt(tokens * n_dp)
    up_tiles = up_all.reshape(groups, K, block_size, block_size)
    down_tiles = down_all.reshape(groups, K, block_size, block_size)
    up_index = up_rows.reshape(groups, K)
    down_index = down_rows.reshape(groups, K)
    x_rows = full_input.reshape(tokens, row_blocks, block_size)
    g_rows = full_grad.reshape(tokens, row_blocks, block_size)
    span = jnp.arange(row_blocks, dtype=jnp.int32)
    up_hot = (up_index[..., None] == span).astype(jnp.bfloat16)
    down_hot = (down_index[..., None] == span).astype(jnp.bfloat16)
    up_dense = jnp.einsum(
        "gkr,gkio->grio", up_hot, up_tiles, preferred_element_type=jnp.float32
    ).astype(jnp.bfloat16)
    down_dense = jnp.einsum(
        "gkr,gkho->ghro", down_hot, down_tiles, preferred_element_type=jnp.float32
    ).astype(jnp.bfloat16)
    preact = jnp.einsum("tri,grio->tgo", x_rows, up_dense, preferred_element_type=jnp.float32)
    hidden = (preact * normal_cdf(preact)).astype(jnp.bfloat16)
    out_part = jnp.einsum("tgh,ghro->tro", hidden, down_dense, preferred_element_type=jnp.float32)
    picked_grad = g_rows[:, down_index]
    down_term = (
        jnp.einsum("tgh,tgko->gkho", hidden, picked_grad, preferred_element_type=jnp.float32)
        * scale
    )
    hidden_grad = jnp.einsum(
        "tro,ghro->tgh", g_rows, down_dense, preferred_element_type=jnp.float32
    )
    preact_grad = (hidden_grad * gelu_slope(preact)).astype(jnp.bfloat16)
    in_part = jnp.einsum("tgo,grio->tri", preact_grad, up_dense, preferred_element_type=jnp.float32)
    picked_in = x_rows[:, up_index]
    up_term = (
        jnp.einsum("tgki,tgo->gkio", picked_in, preact_grad, preferred_element_type=jnp.float32)
        * scale
    )

    parts = jnp.stack([out_part, in_part]).astype(jnp.bfloat16)
    parts = parts.reshape(2, tokens, n_tensor, shard_width)
    mine = scatter_sum(jnp.moveaxis(parts, 2, 0), "tensor")
    both = gather_all(mine, "tensor")
    both = jnp.moveaxis(both, 0, 2).reshape(2, tokens, width)

    terms = jnp.stack([up_term, down_term]).astype(jnp.bfloat16)
    terms = terms.reshape(2, n_y, n_z, per_dev, block_size, block_size)
    grads = dp_scatter_rel(jnp.moveaxis(terms, 0, 2), n_y, n_z)
    return (both[0], both[1], grads[0], grads[1])


def solution(mesh):
    placed = (
        P("dp", "tensor"),
        P("dp", "tensor"),
        P(("tensor", "dp"), None, None),
        P("tensor"),
        P(("tensor", "dp"), None, None),
        P("tensor"),
    )
    return jax.shard_map(
        per_device,
        mesh=mesh,
        in_specs=placed,
        out_specs=(
            P("dp", None),
            P("dp", None),
            P(("tensor", "dp"), None, None),
            P(("tensor", "dp"), None, None),
        ),
        check_vma=False,
    )
```

```python
import math

import jax
import jax.numpy as jnp
from jax import lax
from jax.sharding import PartitionSpec as P

K = 8


def normal_cdf(value):
    return 0.5 * (1.0 + jax.scipy.special.erf(value * 0.7071067811865476))


def gelu_slope(value):
    return normal_cdf(value) + value * jnp.exp(-0.5 * value * value) * 0.3989422804014327


def gather_all(x, axis_name):
    n = lax.axis_size(axis_name)
    spread = jnp.broadcast_to(x[None], (n,) + x.shape)
    return lax.all_to_all(spread, axis_name, 0, 0, tiled=True)


def scatter_sum(x, axis_name):
    got = lax.all_to_all(x, axis_name, 0, 0, tiled=True)
    return got.astype(jnp.float32).sum(axis=0).astype(jnp.bfloat16)


Z_HI = 4


def dp_shift(n_y, n_z, dy, dz):
    return [
        (y * n_z + z, ((y + dy) % n_y) * n_z + (z + dz) % n_z)
        for y in range(n_y)
        for z in range(n_z)
    ]


def dp_gather_rel(x, n_y, n_z):
    by_z = [x] + [lax.ppermute(x, "dp", dp_shift(n_y, n_z, 0, b)) for b in range(1, n_z)]
    held = jnp.stack(by_z)
    n_f, n_b = n_y // 2, (n_y - 1) // 2
    fwd, bwd = [held], []
    cur_f = cur_b = held
    for k in range(1, n_f + 1):
        cur_f = lax.ppermute(cur_f, "dp", dp_shift(n_y, n_z, 1, 0))
        fwd.append(cur_f)
        if k <= n_b:
            cur_b = lax.ppermute(cur_b, "dp", dp_shift(n_y, n_z, -1, 0))
            bwd.append(cur_b)
    rel = fwd + [bwd[n_y - a - 1] for a in range(len(fwd), n_y)]
    return jnp.stack(rel)


def dp_scatter_rel(terms, n_y, n_z):
    n_f, n_b = n_y // 2, (n_y - 1) // 2
    got_f = got_b = None
    for k in range(1, n_f + 1):
        part = terms[(n_y - n_f - 1 + k) % n_y].astype(jnp.float32)
        if got_f is not None:
            part = part + got_f.astype(jnp.float32)
        got_f = lax.ppermute(part.astype(jnp.bfloat16), "dp", dp_shift(n_y, n_z, 1, 0))
    for k in range(1, n_b + 1):
        part = terms[n_b + 1 - k].astype(jnp.float32)
        if got_b is not None:
            part = part + got_b.astype(jnp.float32)
        got_b = lax.ppermute(part.astype(jnp.bfloat16), "dp", dp_shift(n_y, n_z, -1, 0))
    acc = terms[0].astype(jnp.float32)
    if got_f is not None:
        acc = acc + got_f.astype(jnp.float32)
    if got_b is not None:
        acc = acc + got_b.astype(jnp.float32)
    total = acc[0]
    for b in range(1, n_z):
        sent = lax.ppermute(acc[b].astype(jnp.bfloat16), "dp", dp_shift(n_y, n_z, 0, -b))
        total = total + sent.astype(jnp.float32)
    return total.astype(jnp.bfloat16)


def per_device(activations, out_grad, up_blocks, up_rows, down_blocks, down_rows):
    block_size = up_blocks.shape[1]
    groups = up_rows.shape[0] // K
    n_tensor = lax.axis_size("tensor")
    n_dp = lax.axis_size("dp")
    tokens = activations.shape[0]
    shard_width = activations.shape[1]
    width = shard_width * n_tensor
    row_blocks = width // block_size

    feats = gather_all(jnp.stack([activations, out_grad]), "tensor")
    feats = jnp.moveaxis(feats, 0, 2).reshape(2, tokens, width)
    full_input, full_grad = feats[0], feats[1]
    per_dev = up_blocks.shape[0]
    n_z = Z_HI
    n_y = n_dp // n_z
    if n_z * per_dev != K:
        raise ValueError("layout")
    up_all = dp_gather_rel(up_blocks, n_y, n_z).reshape(-1, block_size, block_size)
    down_all = dp_gather_rel(down_blocks, n_y, n_z).reshape(-1, block_size, block_size)
    me = lax.axis_index("dp")
    my_y, my_z = me // n_z, me % n_z
    a = jnp.arange(n_y, dtype=jnp.int32)[:, None, None]
    b = jnp.arange(n_z, dtype=jnp.int32)[None, :, None]
    r = jnp.arange(per_dev, dtype=jnp.int32)[None, None, :]
    order = ((((my_y - a) % n_y) * n_z + (my_z - b) % n_z) * per_dev + r).reshape(-1)
    up_rows = up_rows[order]
    down_rows = down_rows[order]

    scale = 1.0 / math.sqrt(tokens * n_dp)
    up_tiles = up_all.reshape(groups, K, block_size, block_size)
    down_tiles = down_all.reshape(groups, K, block_size, block_size)
    up_index = up_rows.reshape(groups, K)
    down_index = down_rows.reshape(groups, K)
    picked_in = full_input.reshape(tokens, row_blocks, block_size)[:, up_index]
    preact = jnp.einsum("tgki,gkio->tgo", picked_in, up_tiles, preferred_element_type=jnp.float32)
    hidden = (preact * normal_cdf(preact)).astype(jnp.bfloat16)
    product = jnp.einsum("tgh,gkho->tgko", hidden, down_tiles, preferred_element_type=jnp.float32)
    out_start = jnp.zeros((tokens, row_blocks, block_size), jnp.float32)
    out_part = out_start.at[:, down_rows].add(product.reshape(tokens, groups * K, block_size))
    picked_grad = full_grad.reshape(tokens, row_blocks, block_size)[:, down_index]
    down_term = (
        jnp.einsum("tgh,tgko->gkho", hidden, picked_grad, preferred_element_type=jnp.float32)
        * scale
    )
    hidden_grad = jnp.einsum(
        "tgko,gkho->tgh", picked_grad, down_tiles, preferred_element_type=jnp.float32
    )
    preact_grad = (hidden_grad * gelu_slope(preact)).astype(jnp.bfloat16)
    back = jnp.einsum("tgo,gkio->tgki", preact_grad, up_tiles, preferred_element_type=jnp.float32)
    in_start = jnp.zeros((tokens, row_blocks, block_size), jnp.float32)
    in_part = in_start.at[:, up_rows].add(back.reshape(tokens, groups * K, block_size))
    up_term = (
        jnp.einsum("tgki,tgo->gkio", picked_in, preact_grad, preferred_element_type=jnp.float32)
        * scale
    )

    parts = jnp.stack([out_part, in_part]).astype(jnp.bfloat16)
    parts = parts.reshape(2, tokens, n_tensor, shard_width)
    mine = scatter_sum(jnp.moveaxis(parts, 2, 0), "tensor")
    both = gather_all(mine, "tensor")
    both = jnp.moveaxis(both, 0, 2).reshape(2, tokens, width)

    down_sum = dp_scatter_rel(
        down_term.astype(jnp.bfloat16).reshape(n_y, n_z, per_dev, block_size, block_size), n_y, n_z
    )
    up_sum = dp_scatter_rel(
        up_term.astype(jnp.bfloat16).reshape(n_y, n_z, per_dev, block_size, block_size), n_y, n_z
    )
    return (both[0], both[1], up_sum, down_sum)


def solution(mesh):
    placed = (
        P("dp", "tensor"),
        P("dp", "tensor"),
        P(("tensor", "dp"), None, None),
        P("tensor"),
        P(("tensor", "dp"), None, None),
        P("tensor"),
    )
    return jax.shard_map(
        per_device,
        mesh=mesh,
        in_specs=placed,
        out_specs=(
            P("dp", None),
            P("dp", None),
            P(("tensor", "dp"), None, None),
            P(("tensor", "dp"), None, None),
        ),
        check_vma=False,
    )
```

```python
import math

import jax
import jax.numpy as jnp
from jax import lax
from jax.sharding import PartitionSpec as P

K = 8


def normal_cdf(value):
    return 0.5 * (1.0 + jax.scipy.special.erf(value * 0.7071067811865476))


def gelu_slope(value):
    return normal_cdf(value) + value * jnp.exp(-0.5 * value * value) * 0.3989422804014327


def gather_all(x, axis_name):
    n = lax.axis_size(axis_name)
    spread = jnp.broadcast_to(x[None], (n,) + x.shape)
    return lax.all_to_all(spread, axis_name, 0, 0, tiled=True)


def scatter_sum(x, axis_name):
    got = lax.all_to_all(x, axis_name, 0, 0, tiled=True)
    return got.astype(jnp.float32).sum(axis=0).astype(jnp.bfloat16)


Z_HI = 4


def y_shift(n_y, dy):
    return [(y, (y + dy) % n_y) for y in range(n_y)]


def dp_gather_rel(x, n_y):
    held = gather_all(x, "zh")
    n_f, n_b = n_y // 2, (n_y - 1) // 2
    fwd, bwd = [held], []
    cur_f = cur_b = held
    for k in range(1, n_f + 1):
        cur_f = lax.ppermute(cur_f, "y", y_shift(n_y, 1))
        fwd.append(cur_f)
        if k <= n_b:
            cur_b = lax.ppermute(cur_b, "y", y_shift(n_y, -1))
            bwd.append(cur_b)
    rel = fwd + [bwd[n_y - a - 1] for a in range(len(fwd), n_y)]
    return jnp.stack(rel)


def dp_scatter_rel(terms, n_y):
    n_f, n_b = n_y // 2, (n_y - 1) // 2
    got_f = got_b = None
    for k in range(1, n_f + 1):
        part = terms[(n_y - n_f - 1 + k) % n_y].astype(jnp.float32)
        if got_f is not None:
            part = part + got_f.astype(jnp.float32)
        got_f = lax.ppermute(part.astype(jnp.bfloat16), "y", y_shift(n_y, 1))
    for k in range(1, n_b + 1):
        part = terms[n_b + 1 - k].astype(jnp.float32)
        if got_b is not None:
            part = part + got_b.astype(jnp.float32)
        got_b = lax.ppermute(part.astype(jnp.bfloat16), "y", y_shift(n_y, -1))
    acc = terms[0].astype(jnp.float32)
    if got_f is not None:
        acc = acc + got_f.astype(jnp.float32)
    if got_b is not None:
        acc = acc + got_b.astype(jnp.float32)
    return scatter_sum(acc.astype(jnp.bfloat16), "zh")


def per_device(activations, out_grad, up_blocks, up_rows, down_blocks, down_rows):
    block_size = up_blocks.shape[1]
    groups = up_rows.shape[0] // K
    n_tensor = lax.axis_size("tensor")
    n_y = lax.axis_size("y")
    n_z = lax.axis_size("zh")
    n_dp = n_y * n_z
    tokens = activations.shape[0]
    shard_width = activations.shape[1]
    width = shard_width * n_tensor
    row_blocks = width // block_size

    feats = gather_all(jnp.stack([activations, out_grad]), "tensor")
    feats = jnp.moveaxis(feats, 0, 2).reshape(2, tokens, width)
    full_input, full_grad = feats[0], feats[1]
    per_dev = up_blocks.shape[0]
    if n_z * per_dev != K:
        raise ValueError("layout")
    weights = dp_gather_rel(jnp.stack([up_blocks, down_blocks]), n_y)
    weights = jnp.moveaxis(weights, 2, 0).reshape(2, -1, block_size, block_size)
    up_all, down_all = weights[0], weights[1]
    my_y = lax.axis_index("y")
    a = jnp.arange(n_y, dtype=jnp.int32)[:, None, None]
    b = jnp.arange(n_z, dtype=jnp.int32)[None, :, None]
    r = jnp.arange(per_dev, dtype=jnp.int32)[None, None, :]
    order = ((((my_y - a) % n_y) * n_z + b) * per_dev + r).reshape(-1)
    up_rows = up_rows[order]
    down_rows = down_rows[order]

    scale = 1.0 / math.sqrt(tokens * n_dp)
    up_tiles = up_all.reshape(groups, K, block_size, block_size)
    down_tiles = down_all.reshape(groups, K, block_size, block_size)
    up_index = up_rows.reshape(groups, K)
    down_index = down_rows.reshape(groups, K)
    picked_in = full_input.reshape(tokens, row_blocks, block_size)[:, up_index]
    preact = jnp.einsum("tgki,gkio->tgo", picked_in, up_tiles, preferred_element_type=jnp.float32)
    hidden = (preact * normal_cdf(preact)).astype(jnp.bfloat16)
    product = jnp.einsum("tgh,gkho->tgko", hidden, down_tiles, preferred_element_type=jnp.float32)
    out_start = jnp.zeros((tokens, row_blocks, block_size), jnp.float32)
    out_part = out_start.at[:, down_rows].add(product.reshape(tokens, groups * K, block_size))
    picked_grad = full_grad.reshape(tokens, row_blocks, block_size)[:, down_index]
    down_term = (
        jnp.einsum("tgh,tgko->gkho", hidden, picked_grad, preferred_element_type=jnp.float32)
        * scale
    )
    hidden_grad = jnp.einsum(
        "tgko,gkho->tgh", picked_grad, down_tiles, preferred_element_type=jnp.float32
    )
    preact_grad = (hidden_grad * gelu_slope(preact)).astype(jnp.bfloat16)
    back = jnp.einsum("tgo,gkio->tgki", preact_grad, up_tiles, preferred_element_type=jnp.float32)
    in_start = jnp.zeros((tokens, row_blocks, block_size), jnp.float32)
    in_part = in_start.at[:, up_rows].add(back.reshape(tokens, groups * K, block_size))
    up_term = (
        jnp.einsum("tgki,tgo->gkio", picked_in, preact_grad, preferred_element_type=jnp.float32)
        * scale
    )

    parts = jnp.stack([out_part, in_part]).astype(jnp.bfloat16)
    parts = parts.reshape(2, tokens, n_tensor, shard_width)
    mine = scatter_sum(jnp.moveaxis(parts, 2, 0), "tensor")
    both = gather_all(mine, "tensor")
    both = jnp.moveaxis(both, 0, 2).reshape(2, tokens, width)

    terms = jnp.stack([up_term, down_term]).astype(jnp.bfloat16)
    terms = terms.reshape(2, n_y, n_z, per_dev, block_size, block_size)
    grads = dp_scatter_rel(jnp.moveaxis(terms, 0, 2), n_y)
    return (both[0], both[1], grads[0], grads[1])


def solution(mesh):
    n_dp = mesh.shape["dp"]
    n_z = Z_HI if n_dp % Z_HI == 0 else 1
    split = jax.sharding.Mesh(
        mesh.devices.reshape(mesh.shape["tensor"], n_dp // n_z, n_z), ("tensor", "y", "zh")
    )
    dp = ("y", "zh")
    placed = (
        P(dp, "tensor"),
        P(dp, "tensor"),
        P(("tensor",) + dp, None, None),
        P("tensor"),
        P(("tensor",) + dp, None, None),
        P("tensor"),
    )
    return jax.shard_map(
        per_device,
        mesh=split,
        in_specs=placed,
        out_specs=(
            P(dp, None),
            P(dp, None),
            P(("tensor",) + dp, None, None),
            P(("tensor",) + dp, None, None),
        ),
        check_vma=False,
    )
```

```python
import math

import jax
import jax.numpy as jnp
from jax import lax
from jax.sharding import PartitionSpec as P

K = 8


def normal_cdf(value):
    return 0.5 * (1.0 + jax.scipy.special.erf(value * 0.7071067811865476))


def gelu_slope(value):
    return normal_cdf(value) + value * jnp.exp(-0.5 * value * value) * 0.3989422804014327


def gather_all(x, axis_name):
    n = lax.axis_size(axis_name)
    spread = jnp.broadcast_to(x[None], (n,) + x.shape)
    return lax.all_to_all(spread, axis_name, 0, 0, tiled=True)


def scatter_sum(x, axis_name):
    got = lax.all_to_all(x, axis_name, 0, 0, tiled=True)
    return got.astype(jnp.float32).sum(axis=0).astype(jnp.bfloat16)


Z_HI = 4


def dp_shift(n_y, n_z, dy, dz):
    return [
        (y * n_z + z, ((y + dy) % n_y) * n_z + (z + dz) % n_z)
        for y in range(n_y)
        for z in range(n_z)
    ]


def dp_gather_rel(x, n_y, n_z):
    by_z = [x] + [lax.ppermute(x, "dp", dp_shift(n_y, n_z, 0, b)) for b in range(1, n_z)]
    held = jnp.stack(by_z)
    n_f, n_b = n_y // 2, (n_y - 1) // 2
    fwd, bwd = [held], []
    cur_f = cur_b = held
    for k in range(1, n_f + 1):
        cur_f = lax.ppermute(cur_f, "dp", dp_shift(n_y, n_z, 1, 0))
        fwd.append(cur_f)
        if k <= n_b:
            cur_b = lax.ppermute(cur_b, "dp", dp_shift(n_y, n_z, -1, 0))
            bwd.append(cur_b)
    rel = fwd + [bwd[n_y - a - 1] for a in range(len(fwd), n_y)]
    return jnp.stack(rel)


def dp_scatter_rel(terms, n_y, n_z):
    n_f, n_b = n_y // 2, (n_y - 1) // 2
    got_f = got_b = None
    for k in range(1, n_f + 1):
        part = terms[(n_y - n_f - 1 + k) % n_y].astype(jnp.float32)
        if got_f is not None:
            part = part + got_f.astype(jnp.float32)
        got_f = lax.ppermute(part.astype(jnp.bfloat16), "dp", dp_shift(n_y, n_z, 1, 0))
    for k in range(1, n_b + 1):
        part = terms[n_b + 1 - k].astype(jnp.float32)
        if got_b is not None:
            part = part + got_b.astype(jnp.float32)
        got_b = lax.ppermute(part.astype(jnp.bfloat16), "dp", dp_shift(n_y, n_z, -1, 0))
    acc = terms[0].astype(jnp.float32)
    if got_f is not None:
        acc = acc + got_f.astype(jnp.float32)
    if got_b is not None:
        acc = acc + got_b.astype(jnp.float32)
    total = acc[0]
    for b in range(1, n_z):
        sent = lax.ppermute(acc[b].astype(jnp.bfloat16), "dp", dp_shift(n_y, n_z, 0, -b))
        total = total + sent.astype(jnp.float32)
    return total.astype(jnp.bfloat16)


def per_device(activations, out_grad, up_blocks, up_rows, down_blocks, down_rows):
    block_size = up_blocks.shape[1]
    groups = up_rows.shape[0] // K
    n_tensor = lax.axis_size("tensor")
    n_dp = lax.axis_size("dp")
    tokens = activations.shape[0]
    shard_width = activations.shape[1]
    width = shard_width * n_tensor
    row_blocks = width // block_size

    feats = gather_all(jnp.stack([activations, out_grad]), "tensor")
    feats = jnp.moveaxis(feats, 0, 2).reshape(2, tokens, width)
    full_input, full_grad = feats[0], feats[1]
    per_dev = up_blocks.shape[0]
    n_z = Z_HI
    n_y = n_dp // n_z
    if n_z * per_dev != K:
        raise ValueError("layout")
    weights = dp_gather_rel(jnp.stack([up_blocks, down_blocks]), n_y, n_z)
    weights = jnp.moveaxis(weights, 2, 0).reshape(2, -1, block_size, block_size)
    up_all, down_all = weights[0], weights[1]
    me = lax.axis_index("dp")
    my_y, my_z = me // n_z, me % n_z
    a = jnp.arange(n_y, dtype=jnp.int32)[:, None, None]
    b = jnp.arange(n_z, dtype=jnp.int32)[None, :, None]
    r = jnp.arange(per_dev, dtype=jnp.int32)[None, None, :]
    order = ((((my_y - a) % n_y) * n_z + (my_z - b) % n_z) * per_dev + r).reshape(-1)
    up_rows = up_rows[order]
    down_rows = down_rows[order]

    scale = 1.0 / math.sqrt(tokens * n_dp)
    up_tiles = up_all.reshape(groups, K, block_size, block_size)
    down_tiles = down_all.reshape(groups, K, block_size, block_size)
    up_index = up_rows.reshape(groups, K)
    down_index = down_rows.reshape(groups, K)
    picked_in = full_input.reshape(tokens, row_blocks, block_size)[:, up_index]
    preact = jnp.einsum("tgki,gkio->tgo", picked_in, up_tiles, preferred_element_type=jnp.float32)
    hidden = (preact * normal_cdf(preact)).astype(jnp.bfloat16)
    product = jnp.einsum("tgh,gkho->tgko", hidden, down_tiles, preferred_element_type=jnp.float32)
    span = jnp.arange(row_blocks, dtype=jnp.int32)
    highest = lax.Precision.HIGHEST
    down_hot = (down_rows[:, None] == span).astype(jnp.float32)
    out_part = jnp.einsum(
        "tbo,br->tro", product.reshape(tokens, groups * K, block_size), down_hot,
        precision=highest, preferred_element_type=jnp.float32,
    )
    picked_grad = full_grad.reshape(tokens, row_blocks, block_size)[:, down_index]
    down_term = (
        jnp.einsum("tgh,tgko->gkho", hidden, picked_grad, preferred_element_type=jnp.float32)
        * scale
    )
    hidden_grad = jnp.einsum(
        "tgko,gkho->tgh", picked_grad, down_tiles, preferred_element_type=jnp.float32
    )
    preact_grad = (hidden_grad * gelu_slope(preact)).astype(jnp.bfloat16)
    back = jnp.einsum("tgo,gkio->tgki", preact_grad, up_tiles, preferred_element_type=jnp.float32)
    up_hot = (up_rows[:, None] == span).astype(jnp.float32)
    in_part = jnp.einsum(
        "tbi,br->tri", back.reshape(tokens, groups * K, block_size), up_hot,
        precision=highest, preferred_element_type=jnp.float32,
    )
    up_term = (
        jnp.einsum("tgki,tgo->gkio", picked_in, preact_grad, preferred_element_type=jnp.float32)
        * scale
    )

    parts = jnp.stack([out_part, in_part]).astype(jnp.bfloat16)
    parts = parts.reshape(2, tokens, n_tensor, shard_width)
    mine = scatter_sum(jnp.moveaxis(parts, 2, 0), "tensor")
    both = gather_all(mine, "tensor")
    both = jnp.moveaxis(both, 0, 2).reshape(2, tokens, width)

    terms = jnp.stack([up_term, down_term]).astype(jnp.bfloat16)
    terms = terms.reshape(2, n_y, n_z, per_dev, block_size, block_size)
    grads = dp_scatter_rel(jnp.moveaxis(terms, 0, 2), n_y, n_z)
    return (both[0], both[1], grads[0], grads[1])


def solution(mesh):
    placed = (
        P("dp", "tensor"),
        P("dp", "tensor"),
        P(("tensor", "dp"), None, None),
        P("tensor"),
        P(("tensor", "dp"), None, None),
        P("tensor"),
    )
    return jax.shard_map(
        per_device,
        mesh=mesh,
        in_specs=placed,
        out_specs=(
            P("dp", None),
            P("dp", None),
            P(("tensor", "dp"), None, None),
            P(("tensor", "dp"), None, None),
        ),
        check_vma=False,
    )
```

```python
import math

import jax
import jax.numpy as jnp
from jax import lax
from jax.sharding import PartitionSpec as P

K = 8


def normal_cdf(value):
    return 0.5 * (1.0 + jax.scipy.special.erf(value * 0.7071067811865476))


def gelu_slope(value):
    return normal_cdf(value) + value * jnp.exp(-0.5 * value * value) * 0.3989422804014327


def gather_all(x, axis_name):
    n = lax.axis_size(axis_name)
    spread = jnp.broadcast_to(x[None], (n,) + x.shape)
    return lax.all_to_all(spread, axis_name, 0, 0, tiled=True)


def scatter_sum(x, axis_name):
    got = lax.all_to_all(x, axis_name, 0, 0, tiled=True)
    return got.astype(jnp.float32).sum(axis=0).astype(jnp.bfloat16)


Z_HI = 4


def dp_shift(n_y, n_z, dy, dz):
    return [
        (y * n_z + z, ((y + dy) % n_y) * n_z + (z + dz) % n_z)
        for y in range(n_y)
        for z in range(n_z)
    ]


def dp_gather_rel(x, n_y, n_z):
    by_z = [x] + [lax.ppermute(x, "dp", dp_shift(n_y, n_z, 0, b)) for b in range(1, n_z)]
    held = jnp.stack(by_z)
    half = n_y // 2
    split = n_y % 2 == 0 and held.shape[0] % 2 == 0
    cut = held.shape[0] // 2
    piece = {0: held}
    cur = held
    for k in range(1, half + 1):
        if split and k == half:
            fwd_tail = lax.ppermute(cur[:cut], "dp", dp_shift(n_y, n_z, 1, 0))
        else:
            cur = lax.ppermute(cur, "dp", dp_shift(n_y, n_z, 1, 0))
            piece[k] = cur
    cur = held
    for k in range(1, (n_y - 1) // 2 + 1 + int(split)):
        if split and k == half:
            bwd_tail = lax.ppermute(cur[cut:], "dp", dp_shift(n_y, n_z, -1, 0))
        else:
            cur = lax.ppermute(cur, "dp", dp_shift(n_y, n_z, -1, 0))
            piece[n_y - k] = cur
    if split:
        piece[half] = jnp.concatenate([fwd_tail, bwd_tail])
    return jnp.stack([piece[a] for a in range(n_y)])


def ring_chain(terms, n_y, n_z, steps, dest, direction, first):
    got = None
    for k in range(1, steps + 1):
        part = terms[:, dest(k)].astype(jnp.float32)
        if k == 1:
            part = part[:, first]
        elif got is not None:
            if got.shape == part.shape:
                part = part + got.astype(jnp.float32)
            else:
                part = part.at[:, first].add(got.astype(jnp.float32))
        got = lax.ppermute(part.astype(jnp.bfloat16), "dp", dp_shift(n_y, n_z, direction, 0))
    return got


def dp_scatter_rel(terms, n_y, n_z):
    half = n_y // 2
    split = n_y % 2 == 0 and terms.shape[2] % 2 == 0
    cut = terms.shape[2] // 2
    n_b = half if split else (n_y - 1) // 2
    acc = terms[:, 0].astype(jnp.float32)
    if half > 0:
        got_f = ring_chain(
            terms, n_y, n_z, half, lambda k: (n_y - half - 1 + k) % n_y, 1,
            slice(0, cut) if split else slice(None),
        )
        if got_f.shape[1] == acc.shape[1]:
            acc = acc + got_f.astype(jnp.float32)
        else:
            acc = acc.at[:, :cut].add(got_f.astype(jnp.float32))
    if n_b > 0:
        got_b = ring_chain(
            terms, n_y, n_z, n_b, lambda k: n_b + 1 - k, -1,
            slice(cut, None) if split else slice(None),
        )
        if got_b.shape[1] == acc.shape[1]:
            acc = acc + got_b.astype(jnp.float32)
        else:
            acc = acc.at[:, cut:].add(got_b.astype(jnp.float32))
    total = acc[:, 0]
    for b in range(1, n_z):
        sent = lax.ppermute(acc[:, b].astype(jnp.bfloat16), "dp", dp_shift(n_y, n_z, 0, -b))
        total = total + sent.astype(jnp.float32)
    return total.astype(jnp.bfloat16)


def per_device(activations, out_grad, up_blocks, up_rows, down_blocks, down_rows):
    block_size = up_blocks.shape[1]
    groups = up_rows.shape[0] // K
    n_tensor = lax.axis_size("tensor")
    n_dp = lax.axis_size("dp")
    tokens = activations.shape[0]
    shard_width = activations.shape[1]
    width = shard_width * n_tensor
    row_blocks = width // block_size

    feats = gather_all(jnp.stack([activations, out_grad]), "tensor")
    feats = jnp.moveaxis(feats, 0, 2).reshape(2, tokens, width)
    full_input, full_grad = feats[0], feats[1]
    per_dev = up_blocks.shape[0]
    n_z = Z_HI
    n_y = n_dp // n_z
    if n_z * per_dev != K:
        raise ValueError("layout")
    weights = dp_gather_rel(jnp.stack([up_blocks, down_blocks]), n_y, n_z)
    weights = jnp.moveaxis(weights, 2, 0).reshape(2, -1, block_size, block_size)
    up_all, down_all = weights[0], weights[1]
    me = lax.axis_index("dp")
    my_y, my_z = me // n_z, me % n_z
    a = jnp.arange(n_y, dtype=jnp.int32)[:, None, None]
    b = jnp.arange(n_z, dtype=jnp.int32)[None, :, None]
    r = jnp.arange(per_dev, dtype=jnp.int32)[None, None, :]
    order = ((((my_y - a) % n_y) * n_z + (my_z - b) % n_z) * per_dev + r).reshape(-1)
    up_rows = up_rows[order]
    down_rows = down_rows[order]

    scale = 1.0 / math.sqrt(tokens * n_dp)
    up_tiles = up_all.reshape(groups, K, block_size, block_size)
    down_tiles = down_all.reshape(groups, K, block_size, block_size)
    up_index = up_rows.reshape(groups, K)
    down_index = down_rows.reshape(groups, K)
    picked_in = full_input.reshape(tokens, row_blocks, block_size)[:, up_index]
    preact = jnp.einsum("tgki,gkio->tgo", picked_in, up_tiles, preferred_element_type=jnp.float32)
    hidden = (preact * normal_cdf(preact)).astype(jnp.bfloat16)
    product = jnp.einsum("tgh,gkho->tgko", hidden, down_tiles, preferred_element_type=jnp.float32)
    span = jnp.arange(row_blocks, dtype=jnp.int32)
    highest = lax.Precision.HIGHEST
    down_hot = (down_rows[:, None] == span).astype(jnp.float32)
    out_part = jnp.einsum(
        "tbo,br->tro", product.reshape(tokens, groups * K, block_size), down_hot,
        precision=highest, preferred_element_type=jnp.float32,
    )
    picked_grad = full_grad.reshape(tokens, row_blocks, block_size)[:, down_index]
    down_term = (
        jnp.einsum("tgh,tgko->gkho", hidden, picked_grad, preferred_element_type=jnp.float32)
        * scale
    )
    hidden_grad = jnp.einsum(
        "tgko,gkho->tgh", picked_grad, down_tiles, preferred_element_type=jnp.float32
    )
    preact_grad = (hidden_grad * gelu_slope(preact)).astype(jnp.bfloat16)
    back = jnp.einsum("tgo,gkio->tgki", preact_grad, up_tiles, preferred_element_type=jnp.float32)
    up_hot = (up_rows[:, None] == span).astype(jnp.float32)
    in_part = jnp.einsum(
        "tbi,br->tri", back.reshape(tokens, groups * K, block_size), up_hot,
        precision=highest, preferred_element_type=jnp.float32,
    )
    up_term = (
        jnp.einsum("tgki,tgo->gkio", picked_in, preact_grad, preferred_element_type=jnp.float32)
        * scale
    )

    parts = jnp.stack([out_part, in_part]).astype(jnp.bfloat16)
    parts = parts.reshape(2, tokens, n_tensor, shard_width)
    mine = scatter_sum(jnp.moveaxis(parts, 2, 0), "tensor")
    both = gather_all(mine, "tensor")
    both = jnp.moveaxis(both, 0, 2).reshape(2, tokens, width)

    terms = jnp.stack([up_term, down_term]).astype(jnp.bfloat16)
    terms = terms.reshape(2, n_y, n_z, per_dev, block_size, block_size)
    grads = dp_scatter_rel(terms, n_y, n_z)
    return (both[0], both[1], grads[0], grads[1])


def solution(mesh):
    placed = (
        P("dp", "tensor"),
        P("dp", "tensor"),
        P(("tensor", "dp"), None, None),
        P("tensor"),
        P(("tensor", "dp"), None, None),
        P("tensor"),
    )
    return jax.shard_map(
        per_device,
        mesh=mesh,
        in_specs=placed,
        out_specs=(
            P("dp", None),
            P("dp", None),
            P(("tensor", "dp"), None, None),
            P(("tensor", "dp"), None, None),
        ),
        check_vma=False,
    )
```

```python
import math

import jax
import jax.numpy as jnp
from jax import lax
from jax.sharding import PartitionSpec as P

K = 8


def normal_cdf(value):
    return 0.5 * (1.0 + jax.scipy.special.erf(value * 0.7071067811865476))


def gelu_slope(value):
    return normal_cdf(value) + value * jnp.exp(-0.5 * value * value) * 0.3989422804014327


def gather_all(x, axis_name):
    n = lax.axis_size(axis_name)
    spread = jnp.broadcast_to(x[None], (n,) + x.shape)
    return lax.all_to_all(spread, axis_name, 0, 0, tiled=True)


def scatter_sum(x, axis_name):
    got = lax.all_to_all(x, axis_name, 0, 0, tiled=True)
    return got.astype(jnp.float32).sum(axis=0).astype(jnp.bfloat16)


Z_HI = 4


def dp_shift(n_y, n_z, dy, dz):
    return [
        (y * n_z + z, ((y + dy) % n_y) * n_z + (z + dz) % n_z)
        for y in range(n_y)
        for z in range(n_z)
    ]


def dp_gather_rel(x, n_y, n_z):
    by_z = [x] + [lax.ppermute(x, "dp", dp_shift(n_y, n_z, 0, b)) for b in range(1, n_z)]
    held = jnp.stack(by_z)
    n_f, n_b = n_y // 2, (n_y - 1) // 2
    fwd, bwd = [held], []
    cur_f = cur_b = held
    for k in range(1, n_f + 1):
        cur_f = lax.ppermute(cur_f, "dp", dp_shift(n_y, n_z, 1, 0))
        fwd.append(cur_f)
        if k <= n_b:
            cur_b = lax.ppermute(cur_b, "dp", dp_shift(n_y, n_z, -1, 0))
            bwd.append(cur_b)
    rel = fwd + [bwd[n_y - a - 1] for a in range(len(fwd), n_y)]
    return jnp.stack(rel)


def dp_scatter_rel(terms, n_y, n_z):
    n_f, n_b = n_y // 2, (n_y - 1) // 2
    got_f = got_b = None
    for k in range(1, n_f + 1):
        part = terms[(n_y - n_f - 1 + k) % n_y].astype(jnp.float32)
        if got_f is not None:
            part = part + got_f.astype(jnp.float32)
        got_f = lax.ppermute(part.astype(jnp.bfloat16), "dp", dp_shift(n_y, n_z, 1, 0))
    for k in range(1, n_b + 1):
        part = terms[n_b + 1 - k].astype(jnp.float32)
        if got_b is not None:
            part = part + got_b.astype(jnp.float32)
        got_b = lax.ppermute(part.astype(jnp.bfloat16), "dp", dp_shift(n_y, n_z, -1, 0))
    acc = terms[0].astype(jnp.float32)
    if got_f is not None:
        acc = acc + got_f.astype(jnp.float32)
    if got_b is not None:
        acc = acc + got_b.astype(jnp.float32)
    total = acc[0]
    for b in range(1, n_z):
        sent = lax.ppermute(acc[b].astype(jnp.bfloat16), "dp", dp_shift(n_y, n_z, 0, -b))
        total = total + sent.astype(jnp.float32)
    return total.astype(jnp.bfloat16)


def per_device(activations, out_grad, up_blocks, up_rows, down_blocks, down_rows):
    block_size = up_blocks.shape[1]
    groups = up_rows.shape[0] // K
    n_tensor = lax.axis_size("tensor")
    n_dp = lax.axis_size("dp")
    tokens = activations.shape[0]
    shard_width = activations.shape[1]
    width = shard_width * n_tensor
    row_blocks = width // block_size

    feats = gather_all(jnp.stack([activations, out_grad]), "tensor")
    feats = jnp.moveaxis(feats, 0, 2).reshape(2, tokens, width)
    full_input, full_grad = feats[0], feats[1]
    per_dev = up_blocks.shape[0]
    n_z = Z_HI
    n_y = n_dp // n_z
    if n_z * per_dev != K:
        raise ValueError("layout")
    weights = dp_gather_rel(jnp.stack([up_blocks, down_blocks]), n_y, n_z)
    weights = jnp.moveaxis(weights, 2, 0).reshape(2, -1, block_size, block_size)
    up_all, down_all = weights[0], weights[1]
    me = lax.axis_index("dp")
    my_y, my_z = me // n_z, me % n_z
    a = jnp.arange(n_y, dtype=jnp.int32)[:, None, None]
    b = jnp.arange(n_z, dtype=jnp.int32)[None, :, None]
    r = jnp.arange(per_dev, dtype=jnp.int32)[None, None, :]
    order = ((((my_y - a) % n_y) * n_z + (my_z - b) % n_z) * per_dev + r).reshape(-1)
    up_rows = up_rows[order]
    down_rows = down_rows[order]

    scale = 1.0 / math.sqrt(tokens * n_dp)
    up_tiles = up_all.reshape(groups, K, block_size, block_size)
    down_tiles = down_all.reshape(groups, K, block_size, block_size)
    up_index = up_rows.reshape(groups, K)
    down_index = down_rows.reshape(groups, K)
    picked_in = full_input.reshape(tokens, row_blocks, block_size)[:, up_index]
    preact = jnp.einsum("tgki,gkio->tgo", picked_in, up_tiles, preferred_element_type=jnp.float32)
    hidden = (preact * normal_cdf(preact)).astype(jnp.bfloat16)
    product = jnp.einsum("gkho,tgh->gkot", down_tiles, hidden, preferred_element_type=jnp.float32)
    span = jnp.arange(row_blocks, dtype=jnp.int32)
    highest = lax.Precision.HIGHEST
    down_hot = (down_index[..., None] == span).astype(jnp.float32)
    out_t = jnp.einsum(
        "gkr,gkot->rot", down_hot, product, precision=highest, preferred_element_type=jnp.float32
    )
    picked_grad = full_grad.reshape(tokens, row_blocks, block_size)[:, down_index]
    down_term = (
        jnp.einsum("tgh,tgko->gkho", hidden, picked_grad, preferred_element_type=jnp.float32)
        * scale
    )
    hidden_grad = jnp.einsum(
        "tgko,gkho->tgh", picked_grad, down_tiles, preferred_element_type=jnp.float32
    )
    preact_grad = (hidden_grad * gelu_slope(preact)).astype(jnp.bfloat16)
    back = jnp.einsum("gkio,tgo->gkit", up_tiles, preact_grad, preferred_element_type=jnp.float32)
    up_hot = (up_index[..., None] == span).astype(jnp.float32)
    in_t = jnp.einsum(
        "gkr,gkit->rit", up_hot, back, precision=highest, preferred_element_type=jnp.float32
    )
    up_term = (
        jnp.einsum("tgki,tgo->gkio", picked_in, preact_grad, preferred_element_type=jnp.float32)
        * scale
    )

    parts = jnp.stack([out_t, in_t]).astype(jnp.bfloat16)
    parts = parts.reshape(2, n_tensor, shard_width // block_size, block_size, tokens)
    parts = jnp.transpose(parts, (1, 0, 4, 2, 3)).reshape(n_tensor, 2, tokens, shard_width)
    mine = scatter_sum(parts, "tensor")
    both = gather_all(mine, "tensor")
    both = jnp.moveaxis(both, 0, 2).reshape(2, tokens, width)

    terms = jnp.stack([up_term, down_term]).astype(jnp.bfloat16)
    terms = terms.reshape(2, n_y, n_z, per_dev, block_size, block_size)
    grads = dp_scatter_rel(jnp.moveaxis(terms, 0, 2), n_y, n_z)
    return (both[0], both[1], grads[0], grads[1])


def solution(mesh):
    placed = (
        P("dp", "tensor"),
        P("dp", "tensor"),
        P(("tensor", "dp"), None, None),
        P("tensor"),
        P(("tensor", "dp"), None, None),
        P("tensor"),
    )
    return jax.shard_map(
        per_device,
        mesh=mesh,
        in_specs=placed,
        out_specs=(
            P("dp", None),
            P("dp", None),
            P(("tensor", "dp"), None, None),
            P(("tensor", "dp"), None, None),
        ),
        check_vma=False,
    )
```

```python
import math

import jax
import jax.numpy as jnp
from jax import lax
from jax.sharding import PartitionSpec as P

K = 8


def normal_cdf(value):
    return 0.5 * (1.0 + jax.scipy.special.erf(value * 0.7071067811865476))


def gelu_slope(value):
    return normal_cdf(value) + value * jnp.exp(-0.5 * value * value) * 0.3989422804014327


def gather_all(x, axis_name):
    n = lax.axis_size(axis_name)
    spread = jnp.broadcast_to(x[None], (n,) + x.shape)
    return lax.all_to_all(spread, axis_name, 0, 0, tiled=True)


def scatter_sum(x, axis_name):
    got = lax.all_to_all(x, axis_name, 0, 0, tiled=True)
    return got.astype(jnp.float32).sum(axis=0).astype(jnp.bfloat16)


Z_HI = 4


def dp_shift(n_y, n_z, dy, dz):
    return [
        (y * n_z + z, ((y + dy) % n_y) * n_z + (z + dz) % n_z)
        for y in range(n_y)
        for z in range(n_z)
    ]


def dp_gather_rel(x, n_y, n_z):
    by_z = [x] + [lax.ppermute(x, "dp", dp_shift(n_y, n_z, 0, b)) for b in range(1, n_z)]
    held = jnp.stack(by_z)
    n_f, n_b = n_y // 2, (n_y - 1) // 2
    fwd, bwd = [held], []
    cur_f = cur_b = held
    for k in range(1, n_f + 1):
        cur_f = lax.ppermute(cur_f, "dp", dp_shift(n_y, n_z, 1, 0))
        fwd.append(cur_f)
        if k <= n_b:
            cur_b = lax.ppermute(cur_b, "dp", dp_shift(n_y, n_z, -1, 0))
            bwd.append(cur_b)
    rel = fwd + [bwd[n_y - a - 1] for a in range(len(fwd), n_y)]
    return jnp.stack(rel)


def dp_scatter_rel(terms, n_y, n_z):
    n_f, n_b = n_y // 2, (n_y - 1) // 2
    got_f = got_b = None
    for k in range(1, n_f + 1):
        part = terms[(n_y - n_f - 1 + k) % n_y].astype(jnp.float32)
        if got_f is not None:
            part = part + got_f.astype(jnp.float32)
        got_f = lax.ppermute(part.astype(jnp.bfloat16), "dp", dp_shift(n_y, n_z, 1, 0))
    for k in range(1, n_b + 1):
        part = terms[n_b + 1 - k].astype(jnp.float32)
        if got_b is not None:
            part = part + got_b.astype(jnp.float32)
        got_b = lax.ppermute(part.astype(jnp.bfloat16), "dp", dp_shift(n_y, n_z, -1, 0))
    acc = terms[0].astype(jnp.float32)
    if got_f is not None:
        acc = acc + got_f.astype(jnp.float32)
    if got_b is not None:
        acc = acc + got_b.astype(jnp.float32)
    total = acc[0]
    for b in range(1, n_z):
        sent = lax.ppermute(acc[b].astype(jnp.bfloat16), "dp", dp_shift(n_y, n_z, 0, -b))
        total = total + sent.astype(jnp.float32)
    return total.astype(jnp.bfloat16)


def per_device(activations, out_grad, up_blocks, up_rows, down_blocks, down_rows):
    block_size = up_blocks.shape[1]
    groups = up_rows.shape[0] // K
    n_tensor = lax.axis_size("tensor")
    n_dp = lax.axis_size("dp")
    tokens = activations.shape[0]
    shard_width = activations.shape[1]
    width = shard_width * n_tensor
    row_blocks = width // block_size

    feats = gather_all(jnp.stack([activations, out_grad]), "tensor")
    feats = jnp.moveaxis(feats, 0, 2).reshape(2, tokens, width)
    full_input, full_grad = feats[0], feats[1]
    per_dev = up_blocks.shape[0]
    n_z = Z_HI
    n_y = n_dp // n_z
    if n_z * per_dev != K:
        raise ValueError("layout")
    weights = dp_gather_rel(jnp.stack([up_blocks, down_blocks]), n_y, n_z)
    weights = jnp.moveaxis(weights, 2, 0).reshape(2, -1, block_size, block_size)
    up_all, down_all = weights[0], weights[1]
    me = lax.axis_index("dp")
    my_y, my_z = me // n_z, me % n_z
    a = jnp.arange(n_y, dtype=jnp.int32)[:, None, None]
    b = jnp.arange(n_z, dtype=jnp.int32)[None, :, None]
    r = jnp.arange(per_dev, dtype=jnp.int32)[None, None, :]
    order = ((((my_y - a) % n_y) * n_z + (my_z - b) % n_z) * per_dev + r).reshape(-1)
    up_rows = up_rows[order]
    down_rows = down_rows[order]

    scale = 1.0 / math.sqrt(tokens * n_dp)
    up_tiles = up_all.reshape(groups, K, block_size, block_size)
    down_tiles = down_all.reshape(groups, K, block_size, block_size)
    up_index = up_rows.reshape(groups, K)
    down_index = down_rows.reshape(groups, K)
    picked_in = full_input.reshape(tokens, row_blocks, block_size)[:, up_index]
    preact = jnp.einsum("tgki,gkio->tgo", picked_in, up_tiles, preferred_element_type=jnp.float32)
    hidden = (preact * normal_cdf(preact)).astype(jnp.bfloat16)
    spread = jnp.broadcast_to(hidden[:, :, None, :], (tokens, groups, K, block_size))
    product = jnp.einsum("tgkh,gkho->gkto", spread, down_tiles, preferred_element_type=jnp.float32)
    span = jnp.arange(row_blocks, dtype=jnp.int32)
    highest = lax.Precision.HIGHEST
    down_hot = (down_index[..., None] == span).astype(jnp.float32)
    out_t = jnp.einsum(
        "gkr,gkto->rto", down_hot, product, precision=highest, preferred_element_type=jnp.float32
    )
    picked_grad = full_grad.reshape(tokens, row_blocks, block_size)[:, down_index]
    down_term = (
        jnp.einsum("tgh,tgko->gkho", hidden, picked_grad, preferred_element_type=jnp.float32)
        * scale
    )
    hidden_grad = jnp.einsum(
        "tgko,gkho->tgh", picked_grad, down_tiles, preferred_element_type=jnp.float32
    )
    preact_grad = (hidden_grad * gelu_slope(preact)).astype(jnp.bfloat16)
    back = jnp.einsum("gkio,tgo->gkit", up_tiles, preact_grad, preferred_element_type=jnp.float32)
    up_hot = (up_index[..., None] == span).astype(jnp.float32)
    in_t = jnp.einsum(
        "gkr,gkit->rit", up_hot, back, precision=highest, preferred_element_type=jnp.float32
    )
    up_term = (
        jnp.einsum("tgki,tgo->gkio", picked_in, preact_grad, preferred_element_type=jnp.float32)
        * scale
    )

    parts = jnp.stack([out_t, jnp.transpose(in_t, (0, 2, 1))]).astype(jnp.bfloat16)
    parts = parts.reshape(2, n_tensor, shard_width // block_size, tokens, block_size)
    parts = jnp.transpose(parts, (1, 0, 3, 2, 4)).reshape(n_tensor, 2, tokens, shard_width)
    mine = scatter_sum(parts, "tensor")
    both = gather_all(mine, "tensor")
    both = jnp.moveaxis(both, 0, 2).reshape(2, tokens, width)

    terms = jnp.stack([up_term, down_term]).astype(jnp.bfloat16)
    terms = terms.reshape(2, n_y, n_z, per_dev, block_size, block_size)
    grads = dp_scatter_rel(jnp.moveaxis(terms, 0, 2), n_y, n_z)
    return (both[0], both[1], grads[0], grads[1])


def solution(mesh):
    placed = (
        P("dp", "tensor"),
        P("dp", "tensor"),
        P(("tensor", "dp"), None, None),
        P("tensor"),
        P(("tensor", "dp"), None, None),
        P("tensor"),
    )
    return jax.shard_map(
        per_device,
        mesh=mesh,
        in_specs=placed,
        out_specs=(
            P("dp", None),
            P("dp", None),
            P(("tensor", "dp"), None, None),
            P(("tensor", "dp"), None, None),
        ),
        check_vma=False,
    )
```

```python
import math

import jax
import jax.numpy as jnp
from jax import lax
from jax.sharding import PartitionSpec as P

K = 8


def normal_cdf(value):
    return 0.5 * (1.0 + jax.scipy.special.erf(value * 0.7071067811865476))


def gelu_slope(value):
    return normal_cdf(value) + value * jnp.exp(-0.5 * value * value) * 0.3989422804014327


def gather_all(x, axis_name):
    n = lax.axis_size(axis_name)
    spread = jnp.broadcast_to(x[None], (n,) + x.shape)
    return lax.all_to_all(spread, axis_name, 0, 0, tiled=True)


def scatter_sum(x, axis_name):
    got = lax.all_to_all(x, axis_name, 0, 0, tiled=True)
    return got.astype(jnp.float32).sum(axis=0).astype(jnp.bfloat16)


Z_HI = 4


def dp_shift(n_y, n_z, dy, dz):
    return [
        (y * n_z + z, ((y + dy) % n_y) * n_z + (z + dz) % n_z)
        for y in range(n_y)
        for z in range(n_z)
    ]


def dp_gather_rel(x, n_y, n_z):
    by_z = [x] + [lax.ppermute(x, "dp", dp_shift(n_y, n_z, 0, b)) for b in range(1, n_z)]
    held = jnp.stack(by_z)
    n_f, n_b = n_y // 2, (n_y - 1) // 2
    fwd, bwd = [held], []
    cur_f = cur_b = held
    for k in range(1, n_f + 1):
        cur_f = lax.ppermute(cur_f, "dp", dp_shift(n_y, n_z, 1, 0))
        fwd.append(cur_f)
        if k <= n_b:
            cur_b = lax.ppermute(cur_b, "dp", dp_shift(n_y, n_z, -1, 0))
            bwd.append(cur_b)
    rel = fwd + [bwd[n_y - a - 1] for a in range(len(fwd), n_y)]
    return jnp.stack(rel)


def dp_scatter_rel(terms, n_y, n_z, ready=None):
    n_f, n_b = n_y // 2, (n_y - 1) // 2
    got_f = got_b = None
    for k in range(1, n_f + 1):
        part = terms[(n_y - n_f - 1 + k) % n_y].astype(jnp.float32)
        if got_f is not None:
            part = part + got_f.astype(jnp.float32)
        got_f = lax.ppermute(part.astype(jnp.bfloat16), "dp", dp_shift(n_y, n_z, 1, 0))
    for k in range(1, n_b + 1):
        part = terms[n_b + 1 - k].astype(jnp.float32)
        if got_b is not None:
            part = part + got_b.astype(jnp.float32)
        got_b = lax.ppermute(part.astype(jnp.bfloat16), "dp", dp_shift(n_y, n_z, -1, 0))
    acc = terms[0].astype(jnp.float32)
    if got_f is not None:
        acc = acc + got_f.astype(jnp.float32)
    if got_b is not None:
        acc = acc + got_b.astype(jnp.float32)
    if ready is not None:
        acc, ready = lax.optimization_barrier((acc, ready))
    total = acc[0]
    for b in range(1, n_z):
        sent = lax.ppermute(acc[b].astype(jnp.bfloat16), "dp", dp_shift(n_y, n_z, 0, -b))
        total = total + sent.astype(jnp.float32)
    return total.astype(jnp.bfloat16), ready


def per_device(activations, out_grad, up_blocks, up_rows, down_blocks, down_rows):
    block_size = up_blocks.shape[1]
    groups = up_rows.shape[0] // K
    n_tensor = lax.axis_size("tensor")
    n_dp = lax.axis_size("dp")
    tokens = activations.shape[0]
    shard_width = activations.shape[1]
    width = shard_width * n_tensor
    row_blocks = width // block_size

    feats = gather_all(jnp.stack([activations, out_grad]), "tensor")
    feats = jnp.moveaxis(feats, 0, 2).reshape(2, tokens, width)
    full_input, full_grad = feats[0], feats[1]
    per_dev = up_blocks.shape[0]
    n_z = Z_HI
    n_y = n_dp // n_z
    if n_z * per_dev != K:
        raise ValueError("layout")
    weights = dp_gather_rel(jnp.stack([up_blocks, down_blocks]), n_y, n_z)
    weights = jnp.moveaxis(weights, 2, 0).reshape(2, -1, block_size, block_size)
    up_all, down_all = weights[0], weights[1]
    me = lax.axis_index("dp")
    my_y, my_z = me // n_z, me % n_z
    a = jnp.arange(n_y, dtype=jnp.int32)[:, None, None]
    b = jnp.arange(n_z, dtype=jnp.int32)[None, :, None]
    r = jnp.arange(per_dev, dtype=jnp.int32)[None, None, :]
    order = ((((my_y - a) % n_y) * n_z + (my_z - b) % n_z) * per_dev + r).reshape(-1)
    up_rows = up_rows[order]
    down_rows = down_rows[order]

    scale = 1.0 / math.sqrt(tokens * n_dp)
    up_tiles = up_all.reshape(groups, K, block_size, block_size)
    down_tiles = down_all.reshape(groups, K, block_size, block_size)
    up_index = up_rows.reshape(groups, K)
    down_index = down_rows.reshape(groups, K)
    picked_in = full_input.reshape(tokens, row_blocks, block_size)[:, up_index]
    preact = jnp.einsum("tgki,gkio->tgo", picked_in, up_tiles, preferred_element_type=jnp.float32)
    hidden = (preact * normal_cdf(preact)).astype(jnp.bfloat16)
    product = jnp.einsum("gkho,tgh->gkot", down_tiles, hidden, preferred_element_type=jnp.float32)
    span = jnp.arange(row_blocks, dtype=jnp.int32)
    highest = lax.Precision.HIGHEST
    down_hot = (down_index[..., None] == span).astype(jnp.float32)
    out_t = jnp.einsum(
        "gkr,gkot->rot", down_hot, product, precision=highest, preferred_element_type=jnp.float32
    )
    picked_grad = full_grad.reshape(tokens, row_blocks, block_size)[:, down_index]
    down_term = (
        jnp.einsum("tgh,tgko->gkho", hidden, picked_grad, preferred_element_type=jnp.float32)
        * scale
    )
    hidden_grad = jnp.einsum(
        "tgko,gkho->tgh", picked_grad, down_tiles, preferred_element_type=jnp.float32
    )
    preact_grad = (hidden_grad * gelu_slope(preact)).astype(jnp.bfloat16)
    back = jnp.einsum("gkio,tgo->gkit", up_tiles, preact_grad, preferred_element_type=jnp.float32)
    up_hot = (up_index[..., None] == span).astype(jnp.float32)
    in_t = jnp.einsum(
        "gkr,gkit->rit", up_hot, back, precision=highest, preferred_element_type=jnp.float32
    )
    up_term = (
        jnp.einsum("tgki,tgo->gkio", picked_in, preact_grad, preferred_element_type=jnp.float32)
        * scale
    )

    parts = jnp.stack([out_t, in_t]).astype(jnp.bfloat16)
    parts = parts.reshape(2, n_tensor, shard_width // block_size, block_size, tokens)
    parts = jnp.transpose(parts, (1, 0, 4, 2, 3)).reshape(n_tensor, 2, tokens, shard_width)
    mine = scatter_sum(parts, "tensor")
    both = gather_all(mine, "tensor")
    both = jnp.moveaxis(both, 0, 2).reshape(2, tokens, width)
    outs = (both[0], both[1])

    terms = jnp.stack([up_term, down_term]).astype(jnp.bfloat16)
    terms = terms.reshape(2, n_y, n_z, per_dev, block_size, block_size)
    grads, outs = dp_scatter_rel(jnp.moveaxis(terms, 0, 2), n_y, n_z, outs)
    return (outs[0], outs[1], grads[0], grads[1])


def solution(mesh):
    placed = (
        P("dp", "tensor"),
        P("dp", "tensor"),
        P(("tensor", "dp"), None, None),
        P("tensor"),
        P(("tensor", "dp"), None, None),
        P("tensor"),
    )
    return jax.shard_map(
        per_device,
        mesh=mesh,
        in_specs=placed,
        out_specs=(
            P("dp", None),
            P("dp", None),
            P(("tensor", "dp"), None, None),
            P(("tensor", "dp"), None, None),
        ),
        check_vma=False,
    )
```

```python
import math

import jax
import jax.numpy as jnp
from jax import lax
from jax.sharding import PartitionSpec as P

K = 8


def normal_cdf(value):
    return 0.5 * (1.0 + jax.scipy.special.erf(value * 0.7071067811865476))


def gelu_slope(value):
    return normal_cdf(value) + value * jnp.exp(-0.5 * value * value) * 0.3989422804014327


def gather_all(x, axis_name):
    n = lax.axis_size(axis_name)
    spread = jnp.broadcast_to(x[None], (n,) + x.shape)
    return lax.all_to_all(spread, axis_name, 0, 0, tiled=True)


def scatter_sum(x, axis_name):
    got = lax.all_to_all(x, axis_name, 0, 0, tiled=True)
    return got.astype(jnp.float32).sum(axis=0).astype(jnp.bfloat16)


Z_HI = 4


def dp_shift(n_y, n_z, dy, dz):
    return [
        (y * n_z + z, ((y + dy) % n_y) * n_z + (z + dz) % n_z)
        for y in range(n_y)
        for z in range(n_z)
    ]


def dp_gather_rel(x, n_y, n_z, tie=None, tie_step=2):
    by_z = [x] + [lax.ppermute(x, "dp", dp_shift(n_y, n_z, 0, b)) for b in range(1, n_z)]
    held = jnp.stack(by_z)
    n_f, n_b = n_y // 2, (n_y - 1) // 2
    fwd, bwd = [held], []
    cur_f = cur_b = held
    for k in range(1, n_f + 1):
        if tie is not None and k == min(tie_step + 1, n_f):
            cur_f, cur_b, tie = lax.optimization_barrier((cur_f, cur_b, tie))
        cur_f = lax.ppermute(cur_f, "dp", dp_shift(n_y, n_z, 1, 0))
        fwd.append(cur_f)
        if k <= n_b:
            cur_b = lax.ppermute(cur_b, "dp", dp_shift(n_y, n_z, -1, 0))
            bwd.append(cur_b)
    return fwd + [bwd[n_y - a - 1] for a in range(len(fwd), n_y)], tie


def dp_scatter_rel(terms, n_y, n_z):
    n_f, n_b = n_y // 2, (n_y - 1) // 2
    got_f = got_b = None
    for k in range(1, n_f + 1):
        part = terms[(n_y - n_f - 1 + k) % n_y].astype(jnp.float32)
        if got_f is not None:
            part = part + got_f.astype(jnp.float32)
        got_f = lax.ppermute(part.astype(jnp.bfloat16), "dp", dp_shift(n_y, n_z, 1, 0))
    for k in range(1, n_b + 1):
        part = terms[n_b + 1 - k].astype(jnp.float32)
        if got_b is not None:
            part = part + got_b.astype(jnp.float32)
        got_b = lax.ppermute(part.astype(jnp.bfloat16), "dp", dp_shift(n_y, n_z, -1, 0))
    acc = terms[0].astype(jnp.float32)
    if got_f is not None:
        acc = acc + got_f.astype(jnp.float32)
    if got_b is not None:
        acc = acc + got_b.astype(jnp.float32)
    total = acc[0]
    for b in range(1, n_z):
        sent = lax.ppermute(acc[b].astype(jnp.bfloat16), "dp", dp_shift(n_y, n_z, 0, -b))
        total = total + sent.astype(jnp.float32)
    return total.astype(jnp.bfloat16)


def chunk_compute(x_rows, g_rows, pieces, up_rows, down_rows, order_of, scale):
    tokens, row_blocks, block_size = x_rows.shape
    w = jnp.stack(pieces)
    groups = w.shape[0]
    up_tiles = w[:, :, 0].reshape(groups, K, block_size, block_size)
    down_tiles = w[:, :, 1].reshape(groups, K, block_size, block_size)
    up_index = up_rows[order_of].reshape(groups, K)
    down_index = down_rows[order_of].reshape(groups, K)
    picked_in = x_rows[:, up_index]
    preact = jnp.einsum("tgki,gkio->tgo", picked_in, up_tiles, preferred_element_type=jnp.float32)
    hidden = (preact * normal_cdf(preact)).astype(jnp.bfloat16)
    product = jnp.einsum("gkho,tgh->gkot", down_tiles, hidden, preferred_element_type=jnp.float32)
    span = jnp.arange(row_blocks, dtype=jnp.int32)
    highest = lax.Precision.HIGHEST
    down_hot = (down_index[..., None] == span).astype(jnp.float32)
    out_t = jnp.einsum(
        "gkr,gkot->rot", down_hot, product, precision=highest, preferred_element_type=jnp.float32
    )
    picked_grad = g_rows[:, down_index]
    down_term = (
        jnp.einsum("tgh,tgko->gkho", hidden, picked_grad, preferred_element_type=jnp.float32)
        * scale
    )
    hidden_grad = jnp.einsum(
        "tgko,gkho->tgh", picked_grad, down_tiles, preferred_element_type=jnp.float32
    )
    preact_grad = (hidden_grad * gelu_slope(preact)).astype(jnp.bfloat16)
    back = jnp.einsum("gkio,tgo->gkit", up_tiles, preact_grad, preferred_element_type=jnp.float32)
    up_hot = (up_index[..., None] == span).astype(jnp.float32)
    in_t = jnp.einsum(
        "gkr,gkit->rit", up_hot, back, precision=highest, preferred_element_type=jnp.float32
    )
    up_term = (
        jnp.einsum("tgki,tgo->gkio", picked_in, preact_grad, preferred_element_type=jnp.float32)
        * scale
    )
    return out_t, in_t, up_term, down_term


def per_device(activations, out_grad, up_blocks, up_rows, down_blocks, down_rows):
    block_size = up_blocks.shape[1]
    n_tensor = lax.axis_size("tensor")
    n_dp = lax.axis_size("dp")
    tokens = activations.shape[0]
    shard_width = activations.shape[1]
    width = shard_width * n_tensor
    row_blocks = width // block_size

    feats = gather_all(jnp.stack([activations, out_grad]), "tensor")
    per_dev = up_blocks.shape[0]
    n_z = Z_HI
    n_y = n_dp // n_z
    if n_z * per_dev != K:
        raise ValueError("layout")
    pieces, feats = dp_gather_rel(jnp.stack([up_blocks, down_blocks]), n_y, n_z, feats)
    feats = jnp.moveaxis(feats, 0, 2).reshape(2, tokens, width)
    x_rows = feats[0].reshape(tokens, row_blocks, block_size)
    g_rows = feats[1].reshape(tokens, row_blocks, block_size)
    me = lax.axis_index("dp")
    my_y, my_z = me // n_z, me % n_z
    b = jnp.arange(n_z, dtype=jnp.int32)[:, None]
    r = jnp.arange(per_dev, dtype=jnp.int32)[None, :]
    scale = 1.0 / math.sqrt(tokens * n_dp)

    late = [a for a in range(n_y) if min(a, n_y - a) >= n_y // 2 - 1]
    early = [a for a in range(n_y) if a not in late]
    chunks = [c for c in (early, late) if c]
    out_t = in_t = None
    term_of = {}
    for chunk in chunks:
        a = jnp.array(chunk, dtype=jnp.int32)[:, None, None]
        order_of = ((((my_y - a) % n_y) * n_z + (my_z - b) % n_z) * per_dev + r).reshape(-1)
        got = chunk_compute(
            x_rows, g_rows, [pieces[i] for i in chunk], up_rows, down_rows, order_of, scale
        )
        out_t = got[0] if out_t is None else out_t + got[0]
        in_t = got[1] if in_t is None else in_t + got[1]
        up_term = got[2].astype(jnp.bfloat16).reshape(len(chunk), n_z, per_dev, block_size, block_size)
        down_term = got[3].astype(jnp.bfloat16).reshape(len(chunk), n_z, per_dev, block_size, block_size)
        for i, blk in enumerate(chunk):
            term_of[blk] = jnp.stack([up_term[i], down_term[i]], axis=1)

    parts = jnp.stack([out_t, in_t]).astype(jnp.bfloat16)
    parts = parts.reshape(2, n_tensor, shard_width // block_size, block_size, tokens)
    parts = jnp.transpose(parts, (1, 0, 4, 2, 3)).reshape(n_tensor, 2, tokens, shard_width)
    mine = scatter_sum(parts, "tensor")
    both = gather_all(mine, "tensor")
    both = jnp.moveaxis(both, 0, 2).reshape(2, tokens, width)

    grads = dp_scatter_rel([term_of[i] for i in range(n_y)], n_y, n_z)
    return (both[0], both[1], grads[0], grads[1])


def solution(mesh):
    placed = (
        P("dp", "tensor"),
        P("dp", "tensor"),
        P(("tensor", "dp"), None, None),
        P("tensor"),
        P(("tensor", "dp"), None, None),
        P("tensor"),
    )
    return jax.shard_map(
        per_device,
        mesh=mesh,
        in_specs=placed,
        out_specs=(
            P("dp", None),
            P("dp", None),
            P(("tensor", "dp"), None, None),
            P(("tensor", "dp"), None, None),
        ),
        check_vma=False,
    )
```

```python
import math

import jax
import jax.numpy as jnp
from jax import lax
from jax.sharding import PartitionSpec as P

K = 8


def normal_cdf(value):
    return 0.5 * (1.0 + jax.scipy.special.erf(value * 0.7071067811865476))


def gelu_slope(value):
    return normal_cdf(value) + value * jnp.exp(-0.5 * value * value) * 0.3989422804014327


def gather_all(x, axis_name):
    n = lax.axis_size(axis_name)
    spread = jnp.broadcast_to(x[None], (n,) + x.shape)
    return lax.all_to_all(spread, axis_name, 0, 0, tiled=True)


def scatter_sum(x, axis_name):
    got = lax.all_to_all(x, axis_name, 0, 0, tiled=True)
    return got.astype(jnp.float32).sum(axis=0).astype(jnp.bfloat16)


Z_HI = 4


def dp_shift(n_y, n_z, dy, dz):
    return [
        (y * n_z + z, ((y + dy) % n_y) * n_z + (z + dz) % n_z)
        for y in range(n_y)
        for z in range(n_z)
    ]


def dp_gather_rel(x, n_y, n_z):
    by_z = [x] + [lax.ppermute(x, "dp", dp_shift(n_y, n_z, 0, b)) for b in range(1, n_z)]
    held = jnp.stack(by_z)
    n_f, n_b = n_y // 2, (n_y - 1) // 2
    fwd, bwd = [held], []
    cur_f = cur_b = held
    for k in range(1, n_f + 1):
        cur_f = lax.ppermute(cur_f, "dp", dp_shift(n_y, n_z, 1, 0))
        fwd.append(cur_f)
        if k <= n_b:
            cur_b = lax.ppermute(cur_b, "dp", dp_shift(n_y, n_z, -1, 0))
            bwd.append(cur_b)
    rel = fwd + [bwd[n_y - a - 1] for a in range(len(fwd), n_y)]
    return jnp.stack(rel)


def dp_scatter_rel(terms, n_y, n_z, tie=None):
    n_f, n_b = n_y // 2, (n_y - 1) // 2
    got_f = got_b = None
    for k in range(1, n_f + 1):
        part = terms[(n_y - n_f - 1 + k) % n_y].astype(jnp.float32)
        if got_f is not None:
            part = part + got_f.astype(jnp.float32)
        got_f = lax.ppermute(part.astype(jnp.bfloat16), "dp", dp_shift(n_y, n_z, 1, 0))
    for k in range(1, n_b + 1):
        part = terms[n_b + 1 - k].astype(jnp.float32)
        if got_b is not None:
            part = part + got_b.astype(jnp.float32)
        got_b = lax.ppermute(part.astype(jnp.bfloat16), "dp", dp_shift(n_y, n_z, -1, 0))
        if k == 1 and tie is not None:
            got_b, tie = lax.optimization_barrier((got_b, tie))
    acc = terms[0].astype(jnp.float32)
    if got_f is not None:
        acc = acc + got_f.astype(jnp.float32)
    if got_b is not None:
        acc = acc + got_b.astype(jnp.float32)
    total = acc[0]
    for b in range(1, n_z):
        sent = lax.ppermute(acc[b].astype(jnp.bfloat16), "dp", dp_shift(n_y, n_z, 0, -b))
        total = total + sent.astype(jnp.float32)
    return total.astype(jnp.bfloat16), tie


def per_device(activations, out_grad, up_blocks, up_rows, down_blocks, down_rows):
    block_size = up_blocks.shape[1]
    groups = up_rows.shape[0] // K
    n_tensor = lax.axis_size("tensor")
    n_dp = lax.axis_size("dp")
    tokens = activations.shape[0]
    shard_width = activations.shape[1]
    width = shard_width * n_tensor
    row_blocks = width // block_size

    feats = gather_all(jnp.stack([activations, out_grad]), "tensor")
    feats = jnp.moveaxis(feats, 0, 2).reshape(2, tokens, width)
    full_input, full_grad = feats[0], feats[1]
    per_dev = up_blocks.shape[0]
    n_z = Z_HI
    n_y = n_dp // n_z
    if n_z * per_dev != K:
        raise ValueError("layout")
    weights = dp_gather_rel(jnp.stack([up_blocks, down_blocks]), n_y, n_z)
    weights = jnp.moveaxis(weights, 2, 0).reshape(2, -1, block_size, block_size)
    up_all, down_all = weights[0], weights[1]
    me = lax.axis_index("dp")
    my_y, my_z = me // n_z, me % n_z
    a = jnp.arange(n_y, dtype=jnp.int32)[:, None, None]
    b = jnp.arange(n_z, dtype=jnp.int32)[None, :, None]
    r = jnp.arange(per_dev, dtype=jnp.int32)[None, None, :]
    order = ((((my_y - a) % n_y) * n_z + (my_z - b) % n_z) * per_dev + r).reshape(-1)
    up_rows = up_rows[order]
    down_rows = down_rows[order]

    scale = 1.0 / math.sqrt(tokens * n_dp)
    up_tiles = up_all.reshape(groups, K, block_size, block_size)
    down_tiles = down_all.reshape(groups, K, block_size, block_size)
    up_index = up_rows.reshape(groups, K)
    down_index = down_rows.reshape(groups, K)
    picked_in = full_input.reshape(tokens, row_blocks, block_size)[:, up_index]
    preact = jnp.einsum("tgki,gkio->tgo", picked_in, up_tiles, preferred_element_type=jnp.float32)
    hidden = (preact * normal_cdf(preact)).astype(jnp.bfloat16)
    product = jnp.einsum("gkho,tgh->gkot", down_tiles, hidden, preferred_element_type=jnp.float32)
    span = jnp.arange(row_blocks, dtype=jnp.int32)
    highest = lax.Precision.HIGHEST
    down_hot = (down_index[..., None] == span).astype(jnp.float32)
    out_t = jnp.einsum(
        "gkr,gkot->rot", down_hot, product, precision=highest, preferred_element_type=jnp.float32
    )
    picked_grad = full_grad.reshape(tokens, row_blocks, block_size)[:, down_index]
    down_term = (
        jnp.einsum("tgh,tgko->gkho", hidden, picked_grad, preferred_element_type=jnp.float32)
        * scale
    )
    hidden_grad = jnp.einsum(
        "tgko,gkho->tgh", picked_grad, down_tiles, preferred_element_type=jnp.float32
    )
    preact_grad = (hidden_grad * gelu_slope(preact)).astype(jnp.bfloat16)
    back = jnp.einsum("gkio,tgo->gkit", up_tiles, preact_grad, preferred_element_type=jnp.float32)
    up_hot = (up_index[..., None] == span).astype(jnp.float32)
    in_t = jnp.einsum(
        "gkr,gkit->rit", up_hot, back, precision=highest, preferred_element_type=jnp.float32
    )
    up_term = (
        jnp.einsum("tgki,tgo->gkio", picked_in, preact_grad, preferred_element_type=jnp.float32)
        * scale
    )

    parts = jnp.stack([out_t, in_t]).astype(jnp.bfloat16)
    parts = parts.reshape(2, n_tensor, shard_width // block_size, block_size, tokens)
    parts = jnp.transpose(parts, (1, 0, 4, 2, 3)).reshape(n_tensor, 2, tokens, shard_width)
    mine = scatter_sum(parts, "tensor")
    terms = jnp.stack([up_term, down_term]).astype(jnp.bfloat16)
    terms = terms.reshape(2, n_y, n_z, per_dev, block_size, block_size)
    grads, mine = dp_scatter_rel(jnp.moveaxis(terms, 0, 2), n_y, n_z, mine)
    both = gather_all(mine, "tensor")
    both = jnp.moveaxis(both, 0, 2).reshape(2, tokens, width)
    return (both[0], both[1], grads[0], grads[1])


def solution(mesh):
    placed = (
        P("dp", "tensor"),
        P("dp", "tensor"),
        P(("tensor", "dp"), None, None),
        P("tensor"),
        P(("tensor", "dp"), None, None),
        P("tensor"),
    )
    return jax.shard_map(
        per_device,
        mesh=mesh,
        in_specs=placed,
        out_specs=(
            P("dp", None),
            P("dp", None),
            P(("tensor", "dp"), None, None),
            P(("tensor", "dp"), None, None),
        ),
        check_vma=False,
    )
```

```python
import math

import jax
import jax.numpy as jnp
from jax import lax
from jax.sharding import PartitionSpec as P

K = 8


def normal_cdf(value):
    return 0.5 * (1.0 + jax.scipy.special.erf(value * 0.7071067811865476))


def gelu_slope(value):
    return normal_cdf(value) + value * jnp.exp(-0.5 * value * value) * 0.3989422804014327


def gather_all(x, axis_name):
    n = lax.axis_size(axis_name)
    spread = jnp.broadcast_to(x[None], (n,) + x.shape)
    return lax.all_to_all(spread, axis_name, 0, 0, tiled=True)


def scatter_sum(x, axis_name):
    got = lax.all_to_all(x, axis_name, 0, 0, tiled=True)
    return got.astype(jnp.float32).sum(axis=0).astype(jnp.bfloat16)


Z_HI = 4


def dp_shift(n_y, n_z, dy, dz):
    return [
        (y * n_z + z, ((y + dy) % n_y) * n_z + (z + dz) % n_z)
        for y in range(n_y)
        for z in range(n_z)
    ]


def dp_gather_rel(x, n_y, n_z):
    by_z = [x] + [lax.ppermute(x, "dp", dp_shift(n_y, n_z, 0, b)) for b in range(1, n_z)]
    held = jnp.stack(by_z)
    n_f, n_b = n_y // 2, (n_y - 1) // 2
    fwd, bwd = [held], []
    cur_f = cur_b = held
    for k in range(1, n_f + 1):
        cur_f = lax.ppermute(cur_f, "dp", dp_shift(n_y, n_z, 1, 0))
        fwd.append(cur_f)
        if k <= n_b:
            cur_b = lax.ppermute(cur_b, "dp", dp_shift(n_y, n_z, -1, 0))
            bwd.append(cur_b)
    rel = fwd + [bwd[n_y - a - 1] for a in range(len(fwd), n_y)]
    return jnp.stack(rel)


def ring_chain(terms, n_y, n_z, steps, dest, direction, first, tie=None):
    got = None
    for k in range(1, steps + 1):
        part = terms[dest(k)].astype(jnp.float32)
        if k == 1:
            part = part[first]
        elif got.shape == part.shape:
            part = part + got.astype(jnp.float32)
        else:
            part = part.at[first].add(got.astype(jnp.float32))
        got = lax.ppermute(part.astype(jnp.bfloat16), "dp", dp_shift(n_y, n_z, direction, 0))
        if k == 1 and tie is not None:
            got, tie = lax.optimization_barrier((got, tie))
    return got, tie


def dp_scatter_rel(terms, n_y, n_z, tie=None):
    half = n_y // 2
    split = n_y % 2 == 0 and terms.shape[1] % 2 == 0
    cut = terms.shape[1] // 2
    n_b = half if split else (n_y - 1) // 2
    acc = terms[0].astype(jnp.float32)
    for steps, dest, direction, first in (
        (half, lambda k: (n_y - half - 1 + k) % n_y, 1, slice(0, cut) if split else slice(None)),
        (n_b, lambda k: n_b + 1 - k, -1, slice(cut, None) if split else slice(None)),
    ):
        if steps == 0:
            continue
        got, tied = ring_chain(
            terms, n_y, n_z, steps, dest, direction, first, tie if direction < 0 else None
        )
        if direction < 0:
            tie = tied
        if got.shape == acc.shape:
            acc = acc + got.astype(jnp.float32)
        else:
            acc = acc.at[first].add(got.astype(jnp.float32))
    total = acc[0]
    for b in range(1, n_z):
        sent = lax.ppermute(acc[b].astype(jnp.bfloat16), "dp", dp_shift(n_y, n_z, 0, -b))
        total = total + sent.astype(jnp.float32)
    return total.astype(jnp.bfloat16), tie


def per_device(activations, out_grad, up_blocks, up_rows, down_blocks, down_rows):
    block_size = up_blocks.shape[1]
    groups = up_rows.shape[0] // K
    n_tensor = lax.axis_size("tensor")
    n_dp = lax.axis_size("dp")
    tokens = activations.shape[0]
    shard_width = activations.shape[1]
    width = shard_width * n_tensor
    row_blocks = width // block_size

    feats = gather_all(jnp.stack([activations, out_grad]), "tensor")
    feats = jnp.moveaxis(feats, 0, 2).reshape(2, tokens, width)
    full_input, full_grad = feats[0], feats[1]
    per_dev = up_blocks.shape[0]
    n_z = Z_HI
    n_y = n_dp // n_z
    if n_z * per_dev != K:
        raise ValueError("layout")
    weights = dp_gather_rel(jnp.stack([up_blocks, down_blocks]), n_y, n_z)
    weights = jnp.moveaxis(weights, 2, 0).reshape(2, -1, block_size, block_size)
    up_all, down_all = weights[0], weights[1]
    me = lax.axis_index("dp")
    my_y, my_z = me // n_z, me % n_z
    a = jnp.arange(n_y, dtype=jnp.int32)[:, None, None]
    b = jnp.arange(n_z, dtype=jnp.int32)[None, :, None]
    r = jnp.arange(per_dev, dtype=jnp.int32)[None, None, :]
    order = ((((my_y - a) % n_y) * n_z + (my_z - b) % n_z) * per_dev + r).reshape(-1)
    up_rows = up_rows[order]
    down_rows = down_rows[order]

    scale = 1.0 / math.sqrt(tokens * n_dp)
    up_tiles = up_all.reshape(groups, K, block_size, block_size)
    down_tiles = down_all.reshape(groups, K, block_size, block_size)
    up_index = up_rows.reshape(groups, K)
    down_index = down_rows.reshape(groups, K)
    picked_in = full_input.reshape(tokens, row_blocks, block_size)[:, up_index]
    preact = jnp.einsum("tgki,gkio->tgo", picked_in, up_tiles, preferred_element_type=jnp.float32)
    hidden = (preact * normal_cdf(preact)).astype(jnp.bfloat16)
    product = jnp.einsum("gkho,tgh->gkot", down_tiles, hidden, preferred_element_type=jnp.float32)
    span = jnp.arange(row_blocks, dtype=jnp.int32)
    highest = lax.Precision.HIGHEST
    down_hot = (down_index[..., None] == span).astype(jnp.float32)
    out_t = jnp.einsum(
        "gkr,gkot->rot", down_hot, product, precision=highest, preferred_element_type=jnp.float32
    )
    picked_grad = full_grad.reshape(tokens, row_blocks, block_size)[:, down_index]
    down_term = (
        jnp.einsum("tgh,tgko->gkho", hidden, picked_grad, preferred_element_type=jnp.float32)
        * scale
    )
    hidden_grad = jnp.einsum(
        "tgko,gkho->tgh", picked_grad, down_tiles, preferred_element_type=jnp.float32
    )
    preact_grad = (hidden_grad * gelu_slope(preact)).astype(jnp.bfloat16)
    back = jnp.einsum("gkio,tgo->gkit", up_tiles, preact_grad, preferred_element_type=jnp.float32)
    up_hot = (up_index[..., None] == span).astype(jnp.float32)
    in_t = jnp.einsum(
        "gkr,gkit->rit", up_hot, back, precision=highest, preferred_element_type=jnp.float32
    )
    up_term = (
        jnp.einsum("tgki,tgo->gkio", picked_in, preact_grad, preferred_element_type=jnp.float32)
        * scale
    )

    parts = jnp.stack([out_t, in_t]).astype(jnp.bfloat16)
    parts = parts.reshape(2, n_tensor, shard_width // block_size, block_size, tokens)
    parts = jnp.transpose(parts, (1, 0, 4, 2, 3)).reshape(n_tensor, 2, tokens, shard_width)
    mine = scatter_sum(parts, "tensor")
    terms = jnp.stack([up_term, down_term]).astype(jnp.bfloat16)
    terms = terms.reshape(2, n_y, n_z, per_dev, block_size, block_size)
    grads, mine = dp_scatter_rel(jnp.moveaxis(terms, 0, 2), n_y, n_z, mine)
    both = gather_all(mine, "tensor")
    both = jnp.moveaxis(both, 0, 2).reshape(2, tokens, width)
    return (both[0], both[1], grads[0], grads[1])


def solution(mesh):
    placed = (
        P("dp", "tensor"),
        P("dp", "tensor"),
        P(("tensor", "dp"), None, None),
        P("tensor"),
        P(("tensor", "dp"), None, None),
        P("tensor"),
    )
    return jax.shard_map(
        per_device,
        mesh=mesh,
        in_specs=placed,
        out_specs=(
            P("dp", None),
            P("dp", None),
            P(("tensor", "dp"), None, None),
            P(("tensor", "dp"), None, None),
        ),
        check_vma=False,
    )
```

```python
import math

import jax
import jax.numpy as jnp
from jax import lax
from jax.sharding import PartitionSpec as P

K = 8


def normal_cdf(value):
    return 0.5 * (1.0 + jax.scipy.special.erf(value * 0.7071067811865476))


def gelu_slope(value):
    return normal_cdf(value) + value * jnp.exp(-0.5 * value * value) * 0.3989422804014327


def gather_all(x, axis_name):
    n = lax.axis_size(axis_name)
    spread = jnp.broadcast_to(x[None], (n,) + x.shape)
    return lax.all_to_all(spread, axis_name, 0, 0, tiled=True)


def scatter_sum(x, axis_name):
    got = lax.all_to_all(x, axis_name, 0, 0, tiled=True)
    return got.astype(jnp.float32).sum(axis=0).astype(jnp.bfloat16)


Z_HI = 4


def dp_shift(n_y, n_z, dy, dz):
    return [
        (y * n_z + z, ((y + dy) % n_y) * n_z + (z + dz) % n_z)
        for y in range(n_y)
        for z in range(n_z)
    ]


def dp_gather_rel(x, n_y, n_z):
    by_z = [x] + [lax.ppermute(x, "dp", dp_shift(n_y, n_z, 0, b)) for b in range(1, n_z)]
    held = jnp.stack(by_z)
    n_f, n_b = n_y // 2, (n_y - 1) // 2
    fwd, bwd = [held], []
    cur_f = cur_b = held
    for k in range(1, n_f + 1):
        cur_f = lax.ppermute(cur_f, "dp", dp_shift(n_y, n_z, 1, 0))
        fwd.append(cur_f)
        if k <= n_b:
            cur_b = lax.ppermute(cur_b, "dp", dp_shift(n_y, n_z, -1, 0))
            bwd.append(cur_b)
    rel = fwd + [bwd[n_y - a - 1] for a in range(len(fwd), n_y)]
    return jnp.stack(rel)


def dp_scatter_rel(terms, n_y, n_z, late=None):
    n_f, n_b = n_y // 2, (n_y - 1) // 2
    got_f = got_b = None
    made = None
    for k in range(1, n_f + 1):
        part = terms[(n_y - n_f - 1 + k) % n_y].astype(jnp.float32)
        if got_f is not None:
            part = part + got_f.astype(jnp.float32)
        got_f = lax.ppermute(part.astype(jnp.bfloat16), "dp", dp_shift(n_y, n_z, 1, 0))
        if k <= n_b:
            part = terms[n_b + 1 - k].astype(jnp.float32)
            if got_b is not None:
                part = part + got_b.astype(jnp.float32)
            got_b = lax.ppermute(part.astype(jnp.bfloat16), "dp", dp_shift(n_y, n_z, -1, 0))
        if k == 1 and late is not None:
            got_f, got_b, made = late(got_f, got_b)
    acc = terms[0].astype(jnp.float32)
    if got_f is not None:
        acc = acc + got_f.astype(jnp.float32)
    if got_b is not None:
        acc = acc + got_b.astype(jnp.float32)
    total = acc[0]
    for b in range(1, n_z):
        sent = lax.ppermute(acc[b].astype(jnp.bfloat16), "dp", dp_shift(n_y, n_z, 0, -b))
        total = total + sent.astype(jnp.float32)
    return total.astype(jnp.bfloat16), made


def per_device(activations, out_grad, up_blocks, up_rows, down_blocks, down_rows):
    block_size = up_blocks.shape[1]
    groups = up_rows.shape[0] // K
    n_tensor = lax.axis_size("tensor")
    n_dp = lax.axis_size("dp")
    tokens = activations.shape[0]
    shard_width = activations.shape[1]
    width = shard_width * n_tensor
    row_blocks = width // block_size

    feats = gather_all(jnp.stack([activations, out_grad]), "tensor")
    feats = jnp.moveaxis(feats, 0, 2).reshape(2, tokens, width)
    full_input, full_grad = feats[0], feats[1]
    per_dev = up_blocks.shape[0]
    n_z = Z_HI
    n_y = n_dp // n_z
    if n_z * per_dev != K:
        raise ValueError("layout")
    weights = dp_gather_rel(jnp.stack([up_blocks, down_blocks]), n_y, n_z)
    weights = jnp.moveaxis(weights, 2, 0).reshape(2, -1, block_size, block_size)
    up_all, down_all = weights[0], weights[1]
    me = lax.axis_index("dp")
    my_y, my_z = me // n_z, me % n_z
    a = jnp.arange(n_y, dtype=jnp.int32)[:, None, None]
    b = jnp.arange(n_z, dtype=jnp.int32)[None, :, None]
    r = jnp.arange(per_dev, dtype=jnp.int32)[None, None, :]
    order = ((((my_y - a) % n_y) * n_z + (my_z - b) % n_z) * per_dev + r).reshape(-1)
    up_rows = up_rows[order]
    down_rows = down_rows[order]

    scale = 1.0 / math.sqrt(tokens * n_dp)
    up_tiles = up_all.reshape(groups, K, block_size, block_size)
    down_tiles = down_all.reshape(groups, K, block_size, block_size)
    up_index = up_rows.reshape(groups, K)
    down_index = down_rows.reshape(groups, K)
    picked_in = full_input.reshape(tokens, row_blocks, block_size)[:, up_index]
    preact = jnp.einsum("tgki,gkio->tgo", picked_in, up_tiles, preferred_element_type=jnp.float32)
    hidden = (preact * normal_cdf(preact)).astype(jnp.bfloat16)
    picked_grad = full_grad.reshape(tokens, row_blocks, block_size)[:, down_index]
    down_term = (
        jnp.einsum("tgh,tgko->gkho", hidden, picked_grad, preferred_element_type=jnp.float32)
        * scale
    )
    hidden_grad = jnp.einsum(
        "tgko,gkho->tgh", picked_grad, down_tiles, preferred_element_type=jnp.float32
    )
    preact_grad = (hidden_grad * gelu_slope(preact)).astype(jnp.bfloat16)
    up_term = (
        jnp.einsum("tgki,tgo->gkio", picked_in, preact_grad, preferred_element_type=jnp.float32)
        * scale
    )
    terms = jnp.stack([up_term, down_term]).astype(jnp.bfloat16)
    terms = terms.reshape(2, n_y, n_z, per_dev, block_size, block_size)

    def late(got_f, got_b):
        got_f, got_b, h, pg = lax.optimization_barrier((got_f, got_b, hidden, preact_grad))
        product = jnp.einsum("gkho,tgh->gkot", down_tiles, h, preferred_element_type=jnp.float32)
        span = jnp.arange(row_blocks, dtype=jnp.int32)
        highest = lax.Precision.HIGHEST
        down_hot = (down_index[..., None] == span).astype(jnp.float32)
        out_t = jnp.einsum(
            "gkr,gkot->rot", down_hot, product, precision=highest, preferred_element_type=jnp.float32
        )
        back = jnp.einsum("gkio,tgo->gkit", up_tiles, pg, preferred_element_type=jnp.float32)
        up_hot = (up_index[..., None] == span).astype(jnp.float32)
        in_t = jnp.einsum(
            "gkr,gkit->rit", up_hot, back, precision=highest, preferred_element_type=jnp.float32
        )
        parts = jnp.stack([out_t, in_t]).astype(jnp.bfloat16)
        parts = parts.reshape(2, n_tensor, shard_width // block_size, block_size, tokens)
        parts = jnp.transpose(parts, (1, 0, 4, 2, 3)).reshape(n_tensor, 2, tokens, shard_width)
        mine = scatter_sum(parts, "tensor")
        both = gather_all(mine, "tensor")
        return got_f, got_b, jnp.moveaxis(both, 0, 2).reshape(2, tokens, width)

    grads, both = dp_scatter_rel(jnp.moveaxis(terms, 0, 2), n_y, n_z, late)
    return (both[0], both[1], grads[0], grads[1])


def solution(mesh):
    placed = (
        P("dp", "tensor"),
        P("dp", "tensor"),
        P(("tensor", "dp"), None, None),
        P("tensor"),
        P(("tensor", "dp"), None, None),
        P("tensor"),
    )
    return jax.shard_map(
        per_device,
        mesh=mesh,
        in_specs=placed,
        out_specs=(
            P("dp", None),
            P("dp", None),
            P(("tensor", "dp"), None, None),
            P(("tensor", "dp"), None, None),
        ),
        check_vma=False,
    )
```

```python
import math

import jax
import jax.numpy as jnp
from jax import lax
from jax.sharding import PartitionSpec as P

K = 8


def normal_cdf(value):
    return 0.5 * (1.0 + jax.scipy.special.erf(value * 0.7071067811865476))


def gelu_slope(value):
    return normal_cdf(value) + value * jnp.exp(-0.5 * value * value) * 0.3989422804014327


def gather_all(x, axis_name):
    n = lax.axis_size(axis_name)
    spread = jnp.broadcast_to(x[None], (n,) + x.shape)
    return lax.all_to_all(spread, axis_name, 0, 0, tiled=True)


def scatter_sum(x, axis_name):
    got = lax.all_to_all(x, axis_name, 0, 0, tiled=True)
    return got.astype(jnp.float32).sum(axis=0).astype(jnp.bfloat16)


Z_HI = 4


def dp_shift(n_y, n_z, dy, dz):
    return [
        (y * n_z + z, ((y + dy) % n_y) * n_z + (z + dz) % n_z)
        for y in range(n_y)
        for z in range(n_z)
    ]


def dp_gather_rel(x, n_y, n_z):
    by_z = [x] + [lax.ppermute(x, "dp", dp_shift(n_y, n_z, 0, b)) for b in range(1, n_z)]
    held = jnp.stack(by_z)
    n_f, n_b = n_y // 2, (n_y - 1) // 2
    fwd, bwd = [held], []
    cur_f = cur_b = held
    for k in range(1, n_f + 1):
        cur_f = lax.ppermute(cur_f, "dp", dp_shift(n_y, n_z, 1, 0))
        fwd.append(cur_f)
        if k <= n_b:
            cur_b = lax.ppermute(cur_b, "dp", dp_shift(n_y, n_z, -1, 0))
            bwd.append(cur_b)
    rel = fwd + [bwd[n_y - a - 1] for a in range(len(fwd), n_y)]
    return jnp.stack(rel)


def dp_scatter_rel(terms, n_y, n_z, tie=None, after=None):
    n_f, n_b = n_y // 2, (n_y - 1) // 2
    got_f = got_b = None
    for k in range(1, n_f + 1):
        part = terms[(n_y - n_f - 1 + k) % n_y].astype(jnp.float32)
        if got_f is not None:
            part = part + got_f.astype(jnp.float32)
        got_f = lax.ppermute(part.astype(jnp.bfloat16), "dp", dp_shift(n_y, n_z, 1, 0))
    for k in range(1, n_b + 1):
        part = terms[n_b + 1 - k].astype(jnp.float32)
        if got_b is not None:
            part = part + got_b.astype(jnp.float32)
        got_b = lax.ppermute(part.astype(jnp.bfloat16), "dp", dp_shift(n_y, n_z, -1, 0))
        if k == 1 and tie is not None:
            got_b, tie = lax.optimization_barrier((got_b, tie))
            if after is not None:
                tie = after(tie)
    acc = terms[0].astype(jnp.float32)
    if got_f is not None:
        acc = acc + got_f.astype(jnp.float32)
    if got_b is not None:
        acc = acc + got_b.astype(jnp.float32)
    if after is not None:
        acc, tie = lax.optimization_barrier((acc, tie))
    total = acc[0]
    for b in range(1, n_z):
        sent = lax.ppermute(acc[b].astype(jnp.bfloat16), "dp", dp_shift(n_y, n_z, 0, -b))
        total = total + sent.astype(jnp.float32)
    return total.astype(jnp.bfloat16), tie


def per_device(activations, out_grad, up_blocks, up_rows, down_blocks, down_rows):
    block_size = up_blocks.shape[1]
    groups = up_rows.shape[0] // K
    n_tensor = lax.axis_size("tensor")
    n_dp = lax.axis_size("dp")
    tokens = activations.shape[0]
    shard_width = activations.shape[1]
    width = shard_width * n_tensor
    row_blocks = width // block_size

    feats = gather_all(jnp.stack([activations, out_grad]), "tensor")
    feats = jnp.moveaxis(feats, 0, 2).reshape(2, tokens, width)
    full_input, full_grad = feats[0], feats[1]
    per_dev = up_blocks.shape[0]
    n_z = Z_HI
    n_y = n_dp // n_z
    if n_z * per_dev != K:
        raise ValueError("layout")
    weights = dp_gather_rel(jnp.stack([up_blocks, down_blocks]), n_y, n_z)
    weights = jnp.moveaxis(weights, 2, 0).reshape(2, -1, block_size, block_size)
    up_all, down_all = weights[0], weights[1]
    me = lax.axis_index("dp")
    my_y, my_z = me // n_z, me % n_z
    a = jnp.arange(n_y, dtype=jnp.int32)[:, None, None]
    b = jnp.arange(n_z, dtype=jnp.int32)[None, :, None]
    r = jnp.arange(per_dev, dtype=jnp.int32)[None, None, :]
    order = ((((my_y - a) % n_y) * n_z + (my_z - b) % n_z) * per_dev + r).reshape(-1)
    up_rows = up_rows[order]
    down_rows = down_rows[order]

    scale = 1.0 / math.sqrt(tokens * n_dp)
    up_tiles = up_all.reshape(groups, K, block_size, block_size)
    down_tiles = down_all.reshape(groups, K, block_size, block_size)
    up_index = up_rows.reshape(groups, K)
    down_index = down_rows.reshape(groups, K)
    picked_in = full_input.reshape(tokens, row_blocks, block_size)[:, up_index]
    preact = jnp.einsum("tgki,gkio->tgo", picked_in, up_tiles, preferred_element_type=jnp.float32)
    hidden = (preact * normal_cdf(preact)).astype(jnp.bfloat16)
    product = jnp.einsum("gkho,tgh->gkot", down_tiles, hidden, preferred_element_type=jnp.float32)
    span = jnp.arange(row_blocks, dtype=jnp.int32)
    highest = lax.Precision.HIGHEST
    down_hot = (down_index[..., None] == span).astype(jnp.float32)
    out_t = jnp.einsum(
        "gkr,gkot->rot", down_hot, product, precision=highest, preferred_element_type=jnp.float32
    )
    picked_grad = full_grad.reshape(tokens, row_blocks, block_size)[:, down_index]
    down_term = (
        jnp.einsum("tgh,tgko->gkho", hidden, picked_grad, preferred_element_type=jnp.float32)
        * scale
    )
    hidden_grad = jnp.einsum(
        "tgko,gkho->tgh", picked_grad, down_tiles, preferred_element_type=jnp.float32
    )
    preact_grad = (hidden_grad * gelu_slope(preact)).astype(jnp.bfloat16)
    back = jnp.einsum("gkio,tgo->gkit", up_tiles, preact_grad, preferred_element_type=jnp.float32)
    up_hot = (up_index[..., None] == span).astype(jnp.float32)
    in_t = jnp.einsum(
        "gkr,gkit->rit", up_hot, back, precision=highest, preferred_element_type=jnp.float32
    )
    up_term = (
        jnp.einsum("tgki,tgo->gkio", picked_in, preact_grad, preferred_element_type=jnp.float32)
        * scale
    )

    parts = jnp.stack([out_t, in_t]).astype(jnp.bfloat16)
    parts = parts.reshape(2, n_tensor, shard_width // block_size, block_size, tokens)
    parts = jnp.transpose(parts, (1, 0, 4, 2, 3)).reshape(n_tensor, 2, tokens, shard_width)
    mine = scatter_sum(parts, "tensor")
    terms = jnp.stack([up_term, down_term]).astype(jnp.bfloat16)
    terms = terms.reshape(2, n_y, n_z, per_dev, block_size, block_size)
    def outputs(mine):
        both = gather_all(mine, "tensor")
        both = jnp.moveaxis(both, 0, 2).reshape(2, tokens, width)
        return (both[0], both[1])

    grads, outs = dp_scatter_rel(jnp.moveaxis(terms, 0, 2), n_y, n_z, mine, outputs)
    return (outs[0], outs[1], grads[0], grads[1])


def solution(mesh):
    placed = (
        P("dp", "tensor"),
        P("dp", "tensor"),
        P(("tensor", "dp"), None, None),
        P("tensor"),
        P(("tensor", "dp"), None, None),
        P("tensor"),
    )
    return jax.shard_map(
        per_device,
        mesh=mesh,
        in_specs=placed,
        out_specs=(
            P("dp", None),
            P("dp", None),
            P(("tensor", "dp"), None, None),
            P(("tensor", "dp"), None, None),
        ),
        check_vma=False,
    )
```

```python
import math

import jax
import jax.numpy as jnp
from jax import lax
from jax.sharding import PartitionSpec as P

K = 8


def normal_cdf(value):
    return 0.5 * (1.0 + jax.scipy.special.erf(value * 0.7071067811865476))


def gelu_slope(value):
    return normal_cdf(value) + value * jnp.exp(-0.5 * value * value) * 0.3989422804014327


def gather_all(x, axis_name):
    n = lax.axis_size(axis_name)
    spread = jnp.broadcast_to(x[None], (n,) + x.shape)
    return lax.all_to_all(spread, axis_name, 0, 0, tiled=True)


def scatter_sum(x, axis_name):
    got = lax.all_to_all(x, axis_name, 0, 0, tiled=True)
    return got.astype(jnp.float32).sum(axis=0).astype(jnp.bfloat16)


Z_HI = 4


def dp_shift(n_y, n_z, dy, dz):
    return [
        (y * n_z + z, ((y + dy) % n_y) * n_z + (z + dz) % n_z)
        for y in range(n_y)
        for z in range(n_z)
    ]


def dp_gather_rel(x, n_y, n_z):
    by_z = [x] + [lax.ppermute(x, "dp", dp_shift(n_y, n_z, 0, b)) for b in range(1, n_z)]
    held = jnp.stack(by_z)
    n_f, n_b = n_y // 2, (n_y - 1) // 2
    fwd, bwd = [held], []
    cur_f = cur_b = held
    for k in range(1, n_f + 1):
        cur_f = lax.ppermute(cur_f, "dp", dp_shift(n_y, n_z, 1, 0))
        fwd.append(cur_f)
        if k <= n_b:
            cur_b = lax.ppermute(cur_b, "dp", dp_shift(n_y, n_z, -1, 0))
            bwd.append(cur_b)
    rel = fwd + [bwd[n_y - a - 1] for a in range(len(fwd), n_y)]
    return jnp.stack(rel)


def dp_scatter_rel(terms, n_y, n_z, tie=None):
    n_f, n_b = n_y // 2, (n_y - 1) // 2
    got_f = got_b = None
    for k in range(1, n_f + 1):
        part = terms[(n_y - n_f - 1 + k) % n_y].astype(jnp.float32)
        if got_f is not None:
            part = part + got_f.astype(jnp.float32)
        got_f = lax.ppermute(part.astype(jnp.bfloat16), "dp", dp_shift(n_y, n_z, 1, 0))
    for k in range(1, n_b + 1):
        part = terms[n_b + 1 - k].astype(jnp.float32)
        if got_b is not None:
            part = part + got_b.astype(jnp.float32)
        got_b = lax.ppermute(part.astype(jnp.bfloat16), "dp", dp_shift(n_y, n_z, -1, 0))
        if k == min(2, n_b) and tie is not None:
            got_b, tie = lax.optimization_barrier((got_b, tie))
    acc = terms[0].astype(jnp.float32)
    if got_f is not None:
        acc = acc + got_f.astype(jnp.float32)
    if got_b is not None:
        acc = acc + got_b.astype(jnp.float32)
    total = acc[0]
    for b in range(1, n_z):
        sent = lax.ppermute(acc[b].astype(jnp.bfloat16), "dp", dp_shift(n_y, n_z, 0, -b))
        total = total + sent.astype(jnp.float32)
    return total.astype(jnp.bfloat16), tie


def per_device(activations, out_grad, up_blocks, up_rows, down_blocks, down_rows):
    block_size = up_blocks.shape[1]
    groups = up_rows.shape[0] // K
    n_tensor = lax.axis_size("tensor")
    n_dp = lax.axis_size("dp")
    tokens = activations.shape[0]
    shard_width = activations.shape[1]
    width = shard_width * n_tensor
    row_blocks = width // block_size

    feats = gather_all(jnp.stack([activations, out_grad]), "tensor")
    feats = jnp.moveaxis(feats, 0, 2).reshape(2, tokens, width)
    full_input, full_grad = feats[0], feats[1]
    per_dev = up_blocks.shape[0]
    n_z = Z_HI
    n_y = n_dp // n_z
    if n_z * per_dev != K:
        raise ValueError("layout")
    weights = dp_gather_rel(jnp.stack([up_blocks, down_blocks]), n_y, n_z)
    weights = jnp.moveaxis(weights, 2, 0).reshape(2, -1, block_size, block_size)
    up_all, down_all = weights[0], weights[1]
    me = lax.axis_index("dp")
    my_y, my_z = me // n_z, me % n_z
    a = jnp.arange(n_y, dtype=jnp.int32)[:, None, None]
    b = jnp.arange(n_z, dtype=jnp.int32)[None, :, None]
    r = jnp.arange(per_dev, dtype=jnp.int32)[None, None, :]
    order = ((((my_y - a) % n_y) * n_z + (my_z - b) % n_z) * per_dev + r).reshape(-1)
    up_rows = up_rows[order]
    down_rows = down_rows[order]

    scale = 1.0 / math.sqrt(tokens * n_dp)
    up_tiles = up_all.reshape(groups, K, block_size, block_size)
    down_tiles = down_all.reshape(groups, K, block_size, block_size)
    up_index = up_rows.reshape(groups, K)
    down_index = down_rows.reshape(groups, K)
    picked_in = full_input.reshape(tokens, row_blocks, block_size)[:, up_index]
    preact = jnp.einsum("tgki,gkio->tgo", picked_in, up_tiles, preferred_element_type=jnp.float32)
    hidden = (preact * normal_cdf(preact)).astype(jnp.bfloat16)
    product = jnp.einsum("gkho,tgh->gkot", down_tiles, hidden, preferred_element_type=jnp.float32)
    span = jnp.arange(row_blocks, dtype=jnp.int32)
    highest = lax.Precision.HIGHEST
    down_hot = (down_index[..., None] == span).astype(jnp.float32)
    out_t = jnp.einsum(
        "gkr,gkot->rot", down_hot, product, precision=highest, preferred_element_type=jnp.float32
    )
    picked_grad = full_grad.reshape(tokens, row_blocks, block_size)[:, down_index]
    down_term = (
        jnp.einsum("tgh,tgko->gkho", hidden, picked_grad, preferred_element_type=jnp.float32)
        * scale
    )
    hidden_grad = jnp.einsum(
        "tgko,gkho->tgh", picked_grad, down_tiles, preferred_element_type=jnp.float32
    )
    preact_grad = (hidden_grad * gelu_slope(preact)).astype(jnp.bfloat16)
    back = jnp.einsum("gkio,tgo->gkit", up_tiles, preact_grad, preferred_element_type=jnp.float32)
    up_hot = (up_index[..., None] == span).astype(jnp.float32)
    in_t = jnp.einsum(
        "gkr,gkit->rit", up_hot, back, precision=highest, preferred_element_type=jnp.float32
    )
    up_term = (
        jnp.einsum("tgki,tgo->gkio", picked_in, preact_grad, preferred_element_type=jnp.float32)
        * scale
    )

    parts = jnp.stack([out_t, in_t]).astype(jnp.bfloat16)
    parts = parts.reshape(2, n_tensor, shard_width // block_size, block_size, tokens)
    parts = jnp.transpose(parts, (1, 0, 4, 2, 3)).reshape(n_tensor, 2, tokens, shard_width)
    mine = scatter_sum(parts, "tensor")
    terms = jnp.stack([up_term, down_term]).astype(jnp.bfloat16)
    terms = terms.reshape(2, n_y, n_z, per_dev, block_size, block_size)
    grads, mine = dp_scatter_rel(jnp.moveaxis(terms, 0, 2), n_y, n_z, mine)
    both = gather_all(mine, "tensor")
    both = jnp.moveaxis(both, 0, 2).reshape(2, tokens, width)
    return (both[0], both[1], grads[0], grads[1])


def solution(mesh):
    placed = (
        P("dp", "tensor"),
        P("dp", "tensor"),
        P(("tensor", "dp"), None, None),
        P("tensor"),
        P(("tensor", "dp"), None, None),
        P("tensor"),
    )
    return jax.shard_map(
        per_device,
        mesh=mesh,
        in_specs=placed,
        out_specs=(
            P("dp", None),
            P("dp", None),
            P(("tensor", "dp"), None, None),
            P(("tensor", "dp"), None, None),
        ),
        check_vma=False,
    )
```

```python
import math

import jax
import jax.numpy as jnp
from jax import lax
from jax.sharding import PartitionSpec as P

K = 8


def normal_cdf(value):
    return 0.5 * (1.0 + jax.scipy.special.erf(value * 0.7071067811865476))


def gelu_slope(value):
    return normal_cdf(value) + value * jnp.exp(-0.5 * value * value) * 0.3989422804014327


def gather_all(x, axis_name):
    n = lax.axis_size(axis_name)
    spread = jnp.broadcast_to(x[None], (n,) + x.shape)
    return lax.all_to_all(spread, axis_name, 0, 0, tiled=True)


def scatter_sum(x, axis_name):
    got = lax.all_to_all(x, axis_name, 0, 0, tiled=True)
    return got.astype(jnp.float32).sum(axis=0).astype(jnp.bfloat16)


Z_HI = 4


def dp_shift(n_y, n_z, dy, dz):
    return [
        (y * n_z + z, ((y + dy) % n_y) * n_z + (z + dz) % n_z)
        for y in range(n_y)
        for z in range(n_z)
    ]


def dp_gather_rel(x, n_y, n_z):
    by_z = [x] + [lax.ppermute(x, "dp", dp_shift(n_y, n_z, 0, b)) for b in range(1, n_z)]
    held = jnp.stack(by_z)
    n_f, n_b = n_y // 2, (n_y - 1) // 2
    fwd, bwd = [held], []
    cur_f = cur_b = held
    for k in range(1, n_f + 1):
        cur_f = lax.ppermute(cur_f, "dp", dp_shift(n_y, n_z, 1, 0))
        fwd.append(cur_f)
        if k <= n_b:
            cur_b = lax.ppermute(cur_b, "dp", dp_shift(n_y, n_z, -1, 0))
            if k == 1:
                cur_f, cur_b = lax.optimization_barrier((cur_f, cur_b))
                fwd[-1] = cur_f
            bwd.append(cur_b)
    rel = fwd + [bwd[n_y - a - 1] for a in range(len(fwd), n_y)]
    return jnp.stack(rel)


def dp_scatter_rel(terms, n_y, n_z, tie=None):
    n_f, n_b = n_y // 2, (n_y - 1) // 2
    got_f = got_b = None
    for k in range(1, n_f + 1):
        part = terms[(n_y - n_f - 1 + k) % n_y].astype(jnp.float32)
        if got_f is not None:
            part = part + got_f.astype(jnp.float32)
        got_f = lax.ppermute(part.astype(jnp.bfloat16), "dp", dp_shift(n_y, n_z, 1, 0))
    for k in range(1, n_b + 1):
        part = terms[n_b + 1 - k].astype(jnp.float32)
        if got_b is not None:
            part = part + got_b.astype(jnp.float32)
        got_b = lax.ppermute(part.astype(jnp.bfloat16), "dp", dp_shift(n_y, n_z, -1, 0))
        if k == 1 and tie is not None:
            got_b, tie = lax.optimization_barrier((got_b, tie))
    acc = terms[0].astype(jnp.float32)
    if got_f is not None:
        acc = acc + got_f.astype(jnp.float32)
    if got_b is not None:
        acc = acc + got_b.astype(jnp.float32)
    total = acc[0]
    for b in range(1, n_z):
        sent = lax.ppermute(acc[b].astype(jnp.bfloat16), "dp", dp_shift(n_y, n_z, 0, -b))
        total = total + sent.astype(jnp.float32)
    return total.astype(jnp.bfloat16), tie


def per_device(activations, out_grad, up_blocks, up_rows, down_blocks, down_rows):
    block_size = up_blocks.shape[1]
    groups = up_rows.shape[0] // K
    n_tensor = lax.axis_size("tensor")
    n_dp = lax.axis_size("dp")
    tokens = activations.shape[0]
    shard_width = activations.shape[1]
    width = shard_width * n_tensor
    row_blocks = width // block_size

    feats = gather_all(jnp.stack([activations, out_grad]), "tensor")
    feats = jnp.moveaxis(feats, 0, 2).reshape(2, tokens, width)
    full_input, full_grad = feats[0], feats[1]
    per_dev = up_blocks.shape[0]
    n_z = Z_HI
    n_y = n_dp // n_z
    if n_z * per_dev != K:
        raise ValueError("layout")
    weights = dp_gather_rel(jnp.stack([up_blocks, down_blocks]), n_y, n_z)
    weights = jnp.moveaxis(weights, 2, 0).reshape(2, -1, block_size, block_size)
    up_all, down_all = weights[0], weights[1]
    me = lax.axis_index("dp")
    my_y, my_z = me // n_z, me % n_z
    a = jnp.arange(n_y, dtype=jnp.int32)[:, None, None]
    b = jnp.arange(n_z, dtype=jnp.int32)[None, :, None]
    r = jnp.arange(per_dev, dtype=jnp.int32)[None, None, :]
    order = ((((my_y - a) % n_y) * n_z + (my_z - b) % n_z) * per_dev + r).reshape(-1)
    up_rows = up_rows[order]
    down_rows = down_rows[order]

    scale = 1.0 / math.sqrt(tokens * n_dp)
    up_tiles = up_all.reshape(groups, K, block_size, block_size)
    down_tiles = down_all.reshape(groups, K, block_size, block_size)
    up_index = up_rows.reshape(groups, K)
    down_index = down_rows.reshape(groups, K)
    picked_in = full_input.reshape(tokens, row_blocks, block_size)[:, up_index]
    preact = jnp.einsum("tgki,gkio->tgo", picked_in, up_tiles, preferred_element_type=jnp.float32)
    hidden = (preact * normal_cdf(preact)).astype(jnp.bfloat16)
    product = jnp.einsum("gkho,tgh->gkot", down_tiles, hidden, preferred_element_type=jnp.float32)
    span = jnp.arange(row_blocks, dtype=jnp.int32)
    highest = lax.Precision.HIGHEST
    down_hot = (down_index[..., None] == span).astype(jnp.float32)
    out_t = jnp.einsum(
        "gkr,gkot->rot", down_hot, product, precision=highest, preferred_element_type=jnp.float32
    )
    picked_grad = full_grad.reshape(tokens, row_blocks, block_size)[:, down_index]
    down_term = (
        jnp.einsum("tgh,tgko->gkho", hidden, picked_grad, preferred_element_type=jnp.float32)
        * scale
    )
    hidden_grad = jnp.einsum(
        "tgko,gkho->tgh", picked_grad, down_tiles, preferred_element_type=jnp.float32
    )
    preact_grad = (hidden_grad * gelu_slope(preact)).astype(jnp.bfloat16)
    back = jnp.einsum("gkio,tgo->gkit", up_tiles, preact_grad, preferred_element_type=jnp.float32)
    up_hot = (up_index[..., None] == span).astype(jnp.float32)
    in_t = jnp.einsum(
        "gkr,gkit->rit", up_hot, back, precision=highest, preferred_element_type=jnp.float32
    )
    up_term = (
        jnp.einsum("tgki,tgo->gkio", picked_in, preact_grad, preferred_element_type=jnp.float32)
        * scale
    )

    parts = jnp.stack([out_t, in_t]).astype(jnp.bfloat16)
    parts = parts.reshape(2, n_tensor, shard_width // block_size, block_size, tokens)
    parts = jnp.transpose(parts, (1, 0, 4, 2, 3)).reshape(n_tensor, 2, tokens, shard_width)
    mine = scatter_sum(parts, "tensor")
    terms = jnp.stack([up_term, down_term]).astype(jnp.bfloat16)
    terms = terms.reshape(2, n_y, n_z, per_dev, block_size, block_size)
    grads, mine = dp_scatter_rel(jnp.moveaxis(terms, 0, 2), n_y, n_z, mine)
    both = gather_all(mine, "tensor")
    both = jnp.moveaxis(both, 0, 2).reshape(2, tokens, width)
    return (both[0], both[1], grads[0], grads[1])


def solution(mesh):
    placed = (
        P("dp", "tensor"),
        P("dp", "tensor"),
        P(("tensor", "dp"), None, None),
        P("tensor"),
        P(("tensor", "dp"), None, None),
        P("tensor"),
    )
    return jax.shard_map(
        per_device,
        mesh=mesh,
        in_specs=placed,
        out_specs=(
            P("dp", None),
            P("dp", None),
            P(("tensor", "dp"), None, None),
            P(("tensor", "dp"), None, None),
        ),
        check_vma=False,
    )
```
